512 devices in a mesh: pp: 4 (over x_lo, core), cp: 16 (over z, x_hi), tp: 8 (over y).
Axes of the slice: x: 4 (x_hi: 2, x_lo: 2; x = x_hi * 2 + x_lo), y: 8, z: 8, core: 2. Of those that a mesh axis runs over, the one named last changes fastest.
Arguments:
- query: bfloat16 [4, 2048, 16384], P('pp', 'cp', 'tp'), may hold values from -200 to 200
- key: bfloat16 [4, 2048, 1024], P('pp', 'cp', 'tp'), may hold values from -6 to 6
- value: bfloat16 [4, 2048, 1024], P('pp', 'cp', 'tp'), may hold values from -6 to 6
- out_grad: bfloat16 [4, 2048, 16384], P('pp', 'cp', 'tp'), may hold values from -24 to 24
- lengths: int32 [6], replicated, may hold values from 1 to 1024, 2048 in all
- plan: int32 [16, 16], replicated, may hold values from 0 to 15, each once within a row
Outputs:
- handed_grad: bfloat16 [4, 2048, 16384], P('pp', 'cp', 'tp')
- key_grad: bfloat16 [4, 2048, 1024], P('pp', 'cp', 'tp')
- value_grad: bfloat16 [4, 2048, 1024], P('pp', 'cp', 'tp')
The draws below stay inside these ranges and needn't reach their ends.
Inputs may be any that keep to these rules, and one draw needn't show every extreme that they name: Row s of plan is a permutation: for each of the blocks of 8 tokens of context shard s it names the shard that takes the block.
All inputs are finite; a program needn't handle non-finite values.
Results may differ from the reference program's by a relative error of at most 0.0085.
Values may be sent and summed in bfloat16 or wider, within the bound.
No kernel may reach another device: no remote copies, remote signals or barrier semaphores. Data moves between devices by JAX's collectives and lax.ppermute only.
A program may use at most 64 MiB of HBM per device.

```python
import math
import jax
import jax.numpy as jnp
import numpy as np
from jax import lax

HD = 128
NDOC = 6
HEADS = 128
KVH = 8
SEQ = 2048
N_PP = 4
N_CP = 16


def shared_draw(key):
    base = jax.random.fold_in(key, 7)
    key_query, key_key = jax.random.split(base)
    queries = jnp.clip(jax.random.normal(key_query, (N_PP, SEQ, HEADS, HD), jnp.float32), -6.0, 6.0)
    keys = jnp.clip(jax.random.normal(key_key, (N_PP, SEQ, KVH, HD), jnp.float32), -6.0, 6.0)
    return (queries.reshape(N_PP, SEQ, HEADS * HD), keys.reshape(N_PP, SEQ, KVH * HD))


def draw_query(key, part):
    return shared_draw(key)[0].astype(jnp.bfloat16)


def draw_key(key, part):
    return shared_draw(key)[1].astype(jnp.bfloat16)


def block_levels(key, dims, cuts, least, high):
    def one(dim, parts):
        steps = jax.random.uniform(jax.random.fold_in(jax.random.fold_in(key, 6), dim), (parts,), jnp.float32, least / len(cuts), high / len(cuts))
        return jnp.repeat(jnp.exp(steps), dims[dim] // parts).reshape((-1,) + (1,) * (len(dims) - dim - 1))

    factor_of = one(*cuts[0])
    for cut in cuts[1:]:
        factor_of = factor_of * one(*cut)
    return factor_of


def length_profile(number_of, total, reach, lean):
    loads = [(1 << 20) // math.isqrt(rank ** lean) + 1 for rank in range(2, number_of + 1)]
    rest, given = total - reach - (number_of - 1), [1] * (number_of - 1)
    while rest > 0:
        movable = [i for i in range(number_of - 1) if given[i] < reach]
        mass, budget = sum([loads[i] for i in movable]), rest
        for i in movable:
            addition = min(reach - given[i], max(1, budget * loads[i] // mass), rest)
            given[i] = given[i] + addition
            rest = rest - addition
    return np.array([reach] + given)


def uneven(rng, number_of, total, bound, slope):
    if number_of == 2:
        one = jax.random.randint(rng, (), max(1, total - bound), min(bound, total - 1) + 1)
        return jnp.stack([one, total - one])
    sizes = jnp.asarray(length_profile(number_of, total, bound, slope), jnp.int32)
    pairs = (number_of - 1) // 2
    giver, receiver = sizes[1:1 + 2 * pairs:2], sizes[2:2 + 2 * pairs:2]
    slack = jnp.minimum(giver - 1, bound - receiver)
    passed = jax.random.randint(jax.random.fold_in(rng, 1), (pairs,), 0, 1 << 20) % (slack + 1)
    sizes = sizes.at[1:1 + 2 * pairs:2].set(giver - passed).at[2:2 + 2 * pairs:2].set(receiver + passed)
    return sizes[jax.random.permutation(jax.random.fold_in(rng, 2), number_of)]


def noise(own_key, extent, spread, reach, cuts=(), held_as=jnp.bfloat16):
    level = block_levels(own_key, extent, cuts, -0.22, 0.18) if cuts else 1.0
    result = jax.random.normal(own_key, extent, jnp.float32) * spread * level
    return jnp.minimum(jnp.maximum(result, -reach), reach).astype(held_as)


def setup_inputs(seed: int = 0) -> dict:
    streams_of = jax.random.split(jax.random.key(seed), 7)
    return {
        "query": draw_query(jax.random.fold_in(streams_of[6], 71), 0),
        "key": draw_key(jax.random.fold_in(streams_of[6], 71), 0),
        "value": noise(streams_of[2], (N_PP, SEQ, KVH * HD), 1.0, 6.0, ((0, 4), (1, 16), (2, 8))),
        "out_grad": noise(streams_of[3], (N_PP, SEQ, HEADS * HD), 4.0, 24.0, ((0, 4), (1, 16), (2, 8))),
        "lengths": uneven(streams_of[4], NDOC, SEQ, SEQ // 2, 2).astype(jnp.int32),
        "plan": jax.vmap(lambda own: jax.random.permutation(own, N_CP))(jax.random.split(streams_of[5], N_CP)).reshape((N_CP, N_CP)).astype(jnp.int32),
    }


def doc_table(lengths, count):
    ends = jnp.cumsum(lengths).astype(jnp.int32)
    position = jnp.arange(count, dtype=jnp.int32)
    owner = jnp.sum((position[:, None] >= ends[None, :]).astype(jnp.int32), axis=1)
    return owner, position


def reference(query, key, value, out_grad, lengths, plan):
    sections = query.shape[0]
    length = query.shape[1]
    head_count = query.shape[2] // HD
    kv_count = key.shape[2] // HD
    group = head_count // kv_count
    score_scale = HD ** -0.5
    owner, position = doc_table(lengths, length)
    visible = (owner[:, None] == owner[None, :]) & (position[None, :] <= position[:, None])
    visible_rows = jnp.repeat(visible, group, axis=0)

    def one_head(index):
        section = index // kv_count
        kv_head = index % kv_count
        q_section = lax.dynamic_index_in_dim(query, section, 0, keepdims=False)
        g_section = lax.dynamic_index_in_dim(out_grad, section, 0, keepdims=False)
        k_section = lax.dynamic_index_in_dim(key, section, 0, keepdims=False)
        v_section = lax.dynamic_index_in_dim(value, section, 0, keepdims=False)
        q_rows = lax.dynamic_slice_in_dim(q_section, kv_head * group * HD, group * HD, 1).reshape(length * group, HD)
        g_rows = lax.dynamic_slice_in_dim(g_section, kv_head * group * HD, group * HD, 1).reshape(length * group, HD)
        k_rows = lax.dynamic_slice_in_dim(k_section, kv_head * HD, HD, 1)
        v_rows = lax.dynamic_slice_in_dim(v_section, kv_head * HD, HD, 1)
        scores = jnp.dot(q_rows, k_rows.T, preferred_element_type=jnp.float32) * score_scale
        scores = jnp.where(visible_rows, scores, -jnp.inf)
        top = jnp.max(scores, axis=1, keepdims=True)
        expo = jnp.exp(scores - top)
        probs = expo / jnp.sum(expo, axis=1, keepdims=True)
        dprob = jnp.dot(g_rows, v_rows.T, preferred_element_type=jnp.float32)
        delta = jnp.sum(probs * dprob, axis=1, keepdims=True)
        probs_low = probs.astype(jnp.bfloat16)
        dscore = (probs * (dprob - delta) * score_scale).astype(jnp.bfloat16)
        dvalue = jnp.dot(probs_low.T, g_rows, preferred_element_type=jnp.float32)
        dkey = jnp.dot(dscore.T, q_rows, preferred_element_type=jnp.float32)
        dquery = jnp.dot(dscore, k_rows, preferred_element_type=jnp.float32).astype(jnp.bfloat16)
        return dquery.reshape(length, group * HD), dkey.astype(jnp.bfloat16), dvalue.astype(jnp.bfloat16)

    dquery, dkey, dvalue = lax.map(one_head, jnp.arange(sections * kv_count, dtype=jnp.int32))
    dquery = dquery.reshape(sections, kv_count, length, group * HD).transpose(0, 2, 1, 3).reshape(sections, length, head_count * HD)
    dkey = dkey.reshape(sections, kv_count, length, HD).transpose(0, 2, 1, 3).reshape(sections, length, kv_count * HD)
    dvalue = dvalue.reshape(sections, kv_count, length, HD).transpose(0, 2, 1, 3).reshape(sections, length, kv_count * HD)
    shards = plan.shape[0]
    block_rows = length // (shards * shards)
    iota = jnp.arange(shards, dtype=jnp.int32)
    inverse = jnp.sum((plan[:, None, :] == iota[None, :, None]).astype(jnp.int32) * iota[None, None, :], axis=2).astype(jnp.int32)
    natural = dquery.reshape(sections, shards, shards, block_rows, head_count * HD)
    planned = jnp.take_along_axis(natural, inverse[None, :, :, None, None], axis=2)
    planned = planned.transpose(0, 2, 1, 3, 4).reshape(sections, length, head_count * HD)
    handed = jnp.concatenate([planned[1:], jnp.zeros((1, length, head_count * HD), jnp.bfloat16)], axis=0)
    return handed, dkey, dvalue
```

```python
import jax
import jax.numpy as jnp
from jax import lax
from jax.sharding import PartitionSpec as P


def passed_along(array, axis, by):
    peers = lax.axis_size(axis)
    pairs = [(i, i + by) for i in range(peers) if 0 <= i + by < peers]
    return lax.ppermute(array, axis, pairs)


def attend(query_rows, grad_rows, query_pos, key_full, value_full, owner):
    tokens = query_rows.shape[0]
    head_width = key_full.shape[1]
    head_count = query_rows.shape[1] // head_width
    key_count = key_full.shape[0]
    total_rows = tokens * head_count
    score_scale = head_width ** (-0.5)
    flat_query = query_rows.reshape(total_rows, head_width)
    flat_grad = grad_rows.reshape(total_rows, head_width)
    row_pos = jnp.repeat(query_pos, head_count)
    row_doc = jnp.repeat(jnp.take(owner, query_pos), head_count)
    block_width = min(512, key_count)
    block_count = key_count // block_width
    key_pos = jnp.arange(key_count, dtype=jnp.int32)
    blocks = (
        key_full.reshape(block_count, block_width, head_width),
        value_full.reshape(block_count, block_width, head_width),
        key_pos.reshape(block_count, block_width),
        owner.reshape(block_count, block_width),
    )

    def masked_scores(key_block, pos_block, doc_block):
        scores = jnp.dot(flat_query, key_block.T, preferred_element_type=jnp.float32) * score_scale
        seen = (doc_block[None, :] == row_doc[:, None]) & (pos_block[None, :] <= row_pos[:, None])
        return jnp.where(seen, scores, -jnp.inf)

    def first_pass(state, block):
        top, total, weighted = state
        key_block, value_block, pos_block, doc_block = block
        scores = masked_scores(key_block, pos_block, doc_block)
        new_top = jnp.maximum(top, jnp.max(scores, axis=1))
        expo = jnp.exp(scores - new_top[:, None])
        shrink = jnp.exp(top - new_top)
        dprob = jnp.dot(flat_grad, value_block.T, preferred_element_type=jnp.float32)
        total = total * shrink + jnp.sum(expo, axis=1)
        weighted = weighted * shrink + jnp.sum(expo * dprob, axis=1)
        return ((new_top, total, weighted), None)

    start = (
        jnp.full((total_rows,), -1e30, jnp.float32),
        jnp.zeros((total_rows,), jnp.float32),
        jnp.zeros((total_rows,), jnp.float32),
    )
    (top, total, weighted), unused = lax.scan(first_pass, start, blocks)
    delta = weighted / total

    def second_pass(dquery, block):
        key_block, value_block, pos_block, doc_block = block
        scores = masked_scores(key_block, pos_block, doc_block)
        probs = jnp.exp(scores - top[:, None]) / total[:, None]
        dprob = jnp.dot(flat_grad, value_block.T, preferred_element_type=jnp.float32)
        probs_low = probs.astype(jnp.bfloat16)
        dscore = (probs * (dprob - delta[:, None]) * score_scale).astype(jnp.bfloat16)
        dvalue = jnp.dot(probs_low.T, flat_grad, preferred_element_type=jnp.float32)
        dkey = jnp.dot(dscore.T, flat_query, preferred_element_type=jnp.float32)
        dquery = dquery + jnp.dot(dscore, key_block, preferred_element_type=jnp.float32)
        return (dquery, jnp.concatenate([dkey, dvalue], axis=1))

    dquery, terms = lax.scan(second_pass, jnp.zeros((total_rows, head_width), jnp.float32), blocks)
    dquery = dquery.astype(jnp.bfloat16).reshape(tokens, head_count * head_width)
    return (dquery, terms.reshape(key_count, 2 * head_width))


def body(query, key, value, out_grad, lengths, plan):
    tokens = query.shape[1]
    width = query.shape[2]
    head_width = key.shape[2]
    shards = lax.axis_size("cp")
    own_index = lax.axis_index("cp")
    block_rows = tokens // shards
    key_count = shards * tokens
    iota = jnp.arange(shards, dtype=jnp.int32)
    inverse = jnp.sum(
        (plan[:, None, :] == iota[None, :, None]).astype(jnp.int32) * iota[None, None, :], axis=2
    )
    send_order = lax.dynamic_index_in_dim(inverse, own_index, 0, keepdims=False)

    def reorder(rows):
        grouped = rows.reshape(shards, block_rows, rows.shape[1])
        return jnp.take(grouped, send_order, axis=0)

    row_width = block_rows * width
    key_width = tokens * 2 * head_width
    own_keys = jnp.concatenate([key[0], value[0]], axis=1).reshape(1, key_width)
    packed = jnp.concatenate(
        [
            reorder(query[0]).reshape(shards, row_width),
            reorder(out_grad[0]).reshape(shards, row_width),
            jnp.broadcast_to(own_keys, (shards, key_width)),
        ],
        axis=1,
    )
    received = lax.all_to_all(packed, "cp", split_axis=0, concat_axis=0, tiled=True)
    query_sent = received[:, :row_width]
    grad_sent = received[:, row_width : 2 * row_width]
    keys_all = received[:, 2 * row_width :].reshape(key_count, 2 * head_width)
    key_full, value_full = keys_all[:, :head_width], keys_all[:, head_width:]
    ends = jnp.cumsum(lengths)
    positions = jnp.arange(key_count, dtype=jnp.int32)
    owner = jnp.sum((positions[:, None] >= ends[None, :]).astype(jnp.int32), axis=1)
    taken = lax.dynamic_index_in_dim(inverse, own_index, 1, keepdims=False)
    query_pos = (
        iota[:, None] * tokens
        + taken[:, None] * block_rows
        + jnp.arange(block_rows, dtype=jnp.int32)[None, :]
    ).reshape(tokens)
    dquery, terms = attend(
        query_sent.reshape(tokens, width),
        grad_sent.reshape(tokens, width),
        query_pos,
        key_full,
        value_full,
        owner,
    )
    handed = passed_along(dquery, "pp", -1)
    partials = lax.all_to_all(
        terms.reshape(shards, tokens, 2 * head_width), "cp", split_axis=0, concat_axis=0, tiled=True
    )
    summed = jnp.sum(partials, axis=0)
    key_grad = summed[:, :head_width].astype(jnp.bfloat16)
    value_grad = summed[:, head_width:].astype(jnp.bfloat16)
    return (handed[None], key_grad[None], value_grad[None])


def solution(mesh):
    return jax.shard_map(
        body,
        mesh=mesh,
        in_specs=(
            P("pp", "cp", "tp"),
            P("pp", "cp", "tp"),
            P("pp", "cp", "tp"),
            P("pp", "cp", "tp"),
            P(),
            P(),
        ),
        out_specs=(P("pp", "cp", "tp"), P("pp", "cp", "tp"), P("pp", "cp", "tp")),
        check_vma=False,
    )
```

```python
import jax
import jax.numpy as jnp
from jax import lax
from jax.sharding import PartitionSpec as P


def passed_along(array, axis, by):
    peers = lax.axis_size(axis)
    pairs = [(i, i + by) for i in range(peers) if 0 <= i + by < peers]
    return lax.ppermute(array, axis, pairs)


def attend(query_rows, grad_rows, query_pos, key_full, value_full, owner):
    tokens = query_rows.shape[0]
    head_width = key_full.shape[1]
    head_count = query_rows.shape[1] // head_width
    key_count = key_full.shape[0]
    total_rows = tokens * head_count
    score_scale = head_width ** (-0.5)
    flat_query = query_rows.reshape(total_rows, head_width)
    flat_grad = grad_rows.reshape(total_rows, head_width)
    row_pos = jnp.repeat(query_pos, head_count)
    row_doc = jnp.repeat(jnp.take(owner, query_pos), head_count)
    block_width = min(512, key_count)
    block_count = key_count // block_width
    key_pos = jnp.arange(key_count, dtype=jnp.int32)
    blocks = (
        key_full.reshape(block_count, block_width, head_width),
        value_full.reshape(block_count, block_width, head_width),
        key_pos.reshape(block_count, block_width),
        owner.reshape(block_count, block_width),
    )

    def masked_scores(key_block, pos_block, doc_block):
        scores = jnp.dot(flat_query, key_block.T, preferred_element_type=jnp.float32) * score_scale
        seen = (doc_block[None, :] == row_doc[:, None]) & (pos_block[None, :] <= row_pos[:, None])
        return jnp.where(seen, scores, -jnp.inf)

    def first_pass(state, block):
        top, total, weighted = state
        key_block, value_block, pos_block, doc_block = block
        scores = masked_scores(key_block, pos_block, doc_block)
        new_top = jnp.maximum(top, jnp.max(scores, axis=1))
        expo = jnp.exp(scores - new_top[:, None])
        shrink = jnp.exp(top - new_top)
        dprob = jnp.dot(flat_grad, value_block.T, preferred_element_type=jnp.float32)
        total = total * shrink + jnp.sum(expo, axis=1)
        weighted = weighted * shrink + jnp.sum(expo * dprob, axis=1)
        return ((new_top, total, weighted), None)

    start = (
        jnp.full((total_rows,), -1e30, jnp.float32),
        jnp.zeros((total_rows,), jnp.float32),
        jnp.zeros((total_rows,), jnp.float32),
    )
    (top, total, weighted), unused = lax.scan(first_pass, start, blocks)
    delta = weighted / total

    def second_pass(dquery, block):
        key_block, value_block, pos_block, doc_block = block
        scores = masked_scores(key_block, pos_block, doc_block)
        probs = jnp.exp(scores - top[:, None]) / total[:, None]
        dprob = jnp.dot(flat_grad, value_block.T, preferred_element_type=jnp.float32)
        probs_low = probs.astype(jnp.bfloat16)
        dscore = (probs * (dprob - delta[:, None]) * score_scale).astype(jnp.bfloat16)
        dvalue = jnp.dot(probs_low.T, flat_grad, preferred_element_type=jnp.float32)
        dkey = jnp.dot(dscore.T, flat_query, preferred_element_type=jnp.float32)
        dquery = dquery + jnp.dot(dscore, key_block, preferred_element_type=jnp.float32)
        return (dquery, jnp.concatenate([dkey, dvalue], axis=1))

    dquery, terms = lax.scan(second_pass, jnp.zeros((total_rows, head_width), jnp.float32), blocks)
    dquery = dquery.astype(jnp.bfloat16).reshape(tokens, head_count * head_width)
    return (dquery, terms.reshape(key_count, 2 * head_width))


def body(query, key, value, out_grad, lengths, plan):
    tokens = query.shape[1]
    width = query.shape[2]
    head_width = key.shape[2]
    shards = lax.axis_size("cp")
    own_index = lax.axis_index("cp")
    block_rows = tokens // shards
    key_count = shards * tokens
    iota = jnp.arange(shards, dtype=jnp.int32)
    inverse = jnp.sum(
        (plan[:, None, :] == iota[None, :, None]).astype(jnp.int32) * iota[None, None, :], axis=2
    )
    send_order = lax.dynamic_index_in_dim(inverse, own_index, 0, keepdims=False)

    def reorder(rows):
        grouped = rows.reshape(shards, block_rows, rows.shape[1])
        return jnp.take(grouped, send_order, axis=0)

    key_rows = tokens * head_width // width
    own_keys = jnp.concatenate([key[0].reshape(key_rows, width), value[0].reshape(key_rows, width)], axis=0)
    packed = jnp.concatenate(
        [
            reorder(query[0]),
            reorder(out_grad[0]),
            jnp.broadcast_to(own_keys[None], (shards,) + own_keys.shape),
        ],
        axis=1,
    )
    received = lax.all_to_all(packed, "cp", split_axis=0, concat_axis=0, tiled=True)
    query_sent = received[:, :block_rows]
    grad_sent = received[:, block_rows : 2 * block_rows]
    key_at = 2 * block_rows
    key_full = received[:, key_at : key_at + key_rows].reshape(key_count, head_width)
    value_full = received[:, key_at + key_rows :].reshape(key_count, head_width)
    ends = jnp.cumsum(lengths)
    positions = jnp.arange(key_count, dtype=jnp.int32)
    owner = jnp.sum((positions[:, None] >= ends[None, :]).astype(jnp.int32), axis=1)
    taken = lax.dynamic_index_in_dim(inverse, own_index, 1, keepdims=False)
    query_pos = (
        iota[:, None] * tokens
        + taken[:, None] * block_rows
        + jnp.arange(block_rows, dtype=jnp.int32)[None, :]
    ).reshape(tokens)
    dquery, terms = attend(
        query_sent.reshape(tokens, width),
        grad_sent.reshape(tokens, width),
        query_pos,
        key_full,
        value_full,
        owner,
    )
    handed = passed_along(dquery, "pp", -1)
    partials = lax.all_to_all(
        terms.reshape(shards, tokens, 2 * head_width), "cp", split_axis=0, concat_axis=0, tiled=True
    )
    summed = jnp.sum(partials, axis=0)
    key_grad = summed[:, :head_width].astype(jnp.bfloat16)
    value_grad = summed[:, head_width:].astype(jnp.bfloat16)
    return (handed[None], key_grad[None], value_grad[None])


def solution(mesh):
    return jax.shard_map(
        body,
        mesh=mesh,
        in_specs=(
            P("pp", "cp", "tp"),
            P("pp", "cp", "tp"),
            P("pp", "cp", "tp"),
            P("pp", "cp", "tp"),
            P(),
            P(),
        ),
        out_specs=(P("pp", "cp", "tp"), P("pp", "cp", "tp"), P("pp", "cp", "tp")),
        check_vma=False,
    )
```

```python
import functools

import jax
import jax.numpy as jnp
from jax import lax
from jax.sharding import PartitionSpec as P
from jax.experimental import pallas as pl
from jax.experimental.pallas import tpu as pltpu


def passed_along(array, axis, by):
    peers = lax.axis_size(axis)
    pairs = [(i, i + by) for i in range(peers) if 0 <= i + by < peers]
    return lax.ppermute(array, axis, pairs)


def _doc_of(ends_ref, position):
    doc = jnp.int32(0)
    for i in range(ends_ref.shape[0]):
        doc = doc + (position >= ends_ref[i]).astype(jnp.int32)
    return doc


def _attend_kernel(heads, ends_ref, start_ref, q_ref, g_ref, k_ref, v_ref, dq_ref, dkv_ref, top_ref, total_ref, weighted_ref, dq_acc):
    rows, head_width = q_ref.shape
    keys = k_ref.shape[0]
    rb_size = rows // start_ref.shape[0]
    kb_size = 128
    row_blocks = rows // rb_size
    key_blocks = keys // kb_size
    tokens_per_block = rb_size // heads
    scale = head_width ** (-0.5)
    dkv_ref[...] = jnp.zeros_like(dkv_ref)
    row_iota = lax.broadcasted_iota(jnp.int32, (rb_size, kb_size), 0) // heads
    col_iota = lax.broadcasted_iota(jnp.int32, (rb_size, kb_size), 1)

    def vector_doc(position):
        doc = jnp.zeros(position.shape, jnp.int32)
        for i in range(ends_ref.shape[0]):
            doc = doc + (position >= ends_ref[i]).astype(jnp.int32)
        return doc

    def row_block(rb, carry):
        first = start_ref[rb]
        last = first + tokens_per_block - 1
        first_doc = _doc_of(ends_ref, first)
        last_doc = _doc_of(ends_ref, last)
        r0 = pl.multiple_of(rb * rb_size, rb_size)
        q = q_ref[pl.ds(r0, rb_size), :]
        g = g_ref[pl.ds(r0, rb_size), :]
        row_pos = first + row_iota
        row_doc = vector_doc(row_pos)
        top_ref[...] = jnp.full(top_ref.shape, -1e30, jnp.float32)
        total_ref[...] = jnp.zeros(total_ref.shape, jnp.float32)
        weighted_ref[...] = jnp.zeros(weighted_ref.shape, jnp.float32)
        dq_acc[...] = jnp.zeros(dq_acc.shape, jnp.float32)

        def seen(kb):
            k0 = kb * kb_size
            return (k0 <= last) & (_doc_of(ends_ref, k0) <= last_doc) & (_doc_of(ends_ref, k0 + kb_size - 1) >= first_doc)

        def scores_of(kb):
            k0 = pl.multiple_of(kb * kb_size, kb_size)
            k = k_ref[pl.ds(k0, kb_size), :]
            v = v_ref[pl.ds(k0, kb_size), :]
            s = lax.dot_general(q, k, (((1,), (1,)), ((), ())), preferred_element_type=jnp.float32) * scale
            key_pos = k0 + col_iota
            visible = (vector_doc(key_pos) == row_doc) & (key_pos <= row_pos)
            s = jnp.where(visible, s, -jnp.inf)
            dp = lax.dot_general(g, v, (((1,), (1,)), ((), ())), preferred_element_type=jnp.float32)
            return k0, k, s, dp

        def first_pass(kb, c):
            @pl.when(seen(kb))
            def _():
                _, _, s, dp = scores_of(kb)
                top = top_ref[...]
                new_top = jnp.maximum(top, jnp.max(s, axis=1, keepdims=True))
                expo = jnp.exp(s - new_top)
                shrink = jnp.exp(top - new_top)
                total_ref[...] = total_ref[...] * shrink + jnp.sum(expo, axis=1, keepdims=True)
                weighted_ref[...] = weighted_ref[...] * shrink + jnp.sum(expo * dp, axis=1, keepdims=True)
                top_ref[...] = new_top
            return c

        lax.fori_loop(0, key_blocks, first_pass, 0)
        top = top_ref[...]
        total = total_ref[...]
        delta = weighted_ref[...] / total

        def second_pass(kb, c):
            @pl.when(seen(kb))
            def _():
                k0, k, s, dp = scores_of(kb)
                probs = jnp.exp(s - top) / total
                probs_low = probs.astype(jnp.bfloat16)
                dscore = (probs * (dp - delta) * scale).astype(jnp.bfloat16)
                dv = lax.dot_general(probs_low, g, (((0,), (0,)), ((), ())), preferred_element_type=jnp.float32)
                dk = lax.dot_general(dscore, q, (((0,), (0,)), ((), ())), preferred_element_type=jnp.float32)
                dkv_ref[pl.ds(k0, kb_size), pl.ds(0, head_width)] += dk
                dkv_ref[pl.ds(k0, kb_size), pl.ds(head_width, head_width)] += dv
                dq_acc[...] += jnp.dot(dscore, k, preferred_element_type=jnp.float32)
            return c

        lax.fori_loop(0, key_blocks, second_pass, 0)
        dq_ref[pl.ds(r0, rb_size), :] = dq_acc[...].astype(dq_ref.dtype)
        return carry

    lax.fori_loop(0, row_blocks, row_block, 0)


def attend_kernel(flat_query, flat_grad, key_full, value_full, ends, block_start, heads):
    rows, head_width = flat_query.shape
    keys = key_full.shape[0]
    rb_size = rows // block_start.shape[0]
    vmem = pltpu.VMEM
    smem = pl.BlockSpec(memory_space=pltpu.SMEM)
    whole = pl.BlockSpec(memory_space=pltpu.VMEM)
    flops = 2 * rows * keys * head_width * 7
    return pl.pallas_call(
        functools.partial(_attend_kernel, heads),
        out_shape=(
            jax.ShapeDtypeStruct((rows, head_width), jnp.bfloat16),
            jax.ShapeDtypeStruct((keys, 2 * head_width), jnp.float32),
        ),
        in_specs=[smem, smem, whole, whole, whole, whole],
        out_specs=(whole, whole),
        scratch_shapes=[
            vmem((rb_size, 1), jnp.float32),
            vmem((rb_size, 1), jnp.float32),
            vmem((rb_size, 1), jnp.float32),
            vmem((rb_size, head_width), jnp.float32),
        ],
        compiler_params=pltpu.CompilerParams(vmem_limit_bytes=48 * 1024 * 1024),
        cost_estimate=pl.CostEstimate(flops=flops // 4, transcendentals=rows * keys // 2, bytes_accessed=rows * head_width * 6 + keys * head_width * 4 + keys * head_width * 8),
    )(ends, block_start, flat_query, flat_grad, key_full, value_full)


def body(query, key, value, out_grad, lengths, plan):
    tokens = query.shape[1]
    width = query.shape[2]
    head_width = key.shape[2]
    shards = lax.axis_size("cp")
    own_index = lax.axis_index("cp")
    block_rows = tokens // shards
    key_count = shards * tokens
    iota = jnp.arange(shards, dtype=jnp.int32)
    inverse = jnp.sum(
        (plan[:, None, :] == iota[None, :, None]).astype(jnp.int32) * iota[None, None, :], axis=2
    )
    send_order = lax.dynamic_index_in_dim(inverse, own_index, 0, keepdims=False)

    def reorder(rows):
        grouped = rows.reshape(shards, block_rows, rows.shape[1])
        return jnp.take(grouped, send_order, axis=0)

    key_rows = tokens * head_width // width
    own_keys = jnp.concatenate([key[0].reshape(key_rows, width), value[0].reshape(key_rows, width)], axis=0)
    packed = jnp.concatenate(
        [
            reorder(query[0]),
            reorder(out_grad[0]),
            jnp.broadcast_to(own_keys[None], (shards,) + own_keys.shape),
        ],
        axis=1,
    )
    received = lax.all_to_all(packed, "cp", split_axis=0, concat_axis=0, tiled=True)
    query_sent = received[:, :block_rows]
    grad_sent = received[:, block_rows : 2 * block_rows]
    key_at = 2 * block_rows
    key_full = received[:, key_at : key_at + key_rows].reshape(key_count, head_width)
    value_full = received[:, key_at + key_rows :].reshape(key_count, head_width)
    ends = jnp.cumsum(lengths).astype(jnp.int32)
    taken = lax.dynamic_index_in_dim(inverse, own_index, 1, keepdims=False)
    head_count = width // head_width
    dquery, terms = attend_kernel(
        query_sent.reshape(tokens * head_count, head_width),
        grad_sent.reshape(tokens * head_count, head_width),
        key_full,
        value_full,
        ends,
        iota * tokens + taken * block_rows,
        head_count,
    )
    dquery = dquery.reshape(tokens, width)
    handed = passed_along(dquery, "pp", -1)
    partials = lax.all_to_all(
        terms.reshape(shards, tokens, 2 * head_width), "cp", split_axis=0, concat_axis=0, tiled=True
    )
    summed = jnp.sum(partials, axis=0)
    key_grad = summed[:, :head_width].astype(jnp.bfloat16)
    value_grad = summed[:, head_width:].astype(jnp.bfloat16)
    return (handed[None], key_grad[None], value_grad[None])


def solution(mesh):
    return jax.shard_map(
        body,
        mesh=mesh,
        in_specs=(
            P("pp", "cp", "tp"),
            P("pp", "cp", "tp"),
            P("pp", "cp", "tp"),
            P("pp", "cp", "tp"),
            P(),
            P(),
        ),
        out_specs=(P("pp", "cp", "tp"), P("pp", "cp", "tp"), P("pp", "cp", "tp")),
        check_vma=False,
    )
```

```python
import functools

import jax
import jax.numpy as jnp
from jax import lax
from jax.sharding import PartitionSpec as P
from jax.experimental import pallas as pl
from jax.experimental.pallas import tpu as pltpu


def passed_along(array, axis, by):
    peers = lax.axis_size(axis)
    pairs = [(i, i + by) for i in range(peers) if 0 <= i + by < peers]
    return lax.ppermute(array, axis, pairs)


def _doc_of(ends_ref, position):
    doc = jnp.int32(0)
    for i in range(ends_ref.shape[0]):
        doc = doc + (position >= ends_ref[i]).astype(jnp.int32)
    return doc


def _attend_kernel(heads, kb_size, ends_ref, start_ref, kdoc_ref, q_ref, g_ref, k_ref, v_ref, dq_ref, dkv_ref, top_ref, total_ref, weighted_ref, dq_acc):
    rows, head_width = q_ref.shape
    keys = k_ref.shape[0]
    rb_size = rows // start_ref.shape[0]
    row_blocks = rows // rb_size
    key_blocks = keys // kb_size
    tokens_per_block = rb_size // heads
    scale = head_width ** (-0.5)
    dkv_ref[...] = jnp.zeros_like(dkv_ref)
    row_iota = lax.broadcasted_iota(jnp.int32, (rb_size, kb_size), 0) // heads
    col_iota = lax.broadcasted_iota(jnp.int32, (rb_size, kb_size), 1)
    row_iota1 = lax.broadcasted_iota(jnp.int32, (rb_size, 1), 0) // heads

    def vector_doc(position):
        doc = jnp.zeros(position.shape, jnp.int32)
        for i in range(ends_ref.shape[0]):
            doc = doc + (position >= ends_ref[i]).astype(jnp.int32)
        return doc

    def row_block(rb, carry):
        first = start_ref[rb]
        last = first + tokens_per_block - 1
        first_doc = _doc_of(ends_ref, first)
        last_doc = _doc_of(ends_ref, last)
        r0 = pl.multiple_of(rb * rb_size, rb_size)
        q = q_ref[pl.ds(r0, rb_size), :]
        g = g_ref[pl.ds(r0, rb_size), :]
        row_pos = first + row_iota
        row_doc = vector_doc(first + row_iota1)
        top_ref[...] = jnp.full(top_ref.shape, -1e30, jnp.float32)
        total_ref[...] = jnp.zeros(total_ref.shape, jnp.float32)
        weighted_ref[...] = jnp.zeros(weighted_ref.shape, jnp.float32)
        dq_acc[...] = jnp.zeros(dq_acc.shape, jnp.float32)

        def seen(kb):
            k0 = kb * kb_size
            return (k0 <= last) & (_doc_of(ends_ref, k0) <= last_doc) & (_doc_of(ends_ref, k0 + kb_size - 1) >= first_doc)

        def scores_of(kb):
            k0 = pl.multiple_of(kb * kb_size, kb_size)
            k = k_ref[pl.ds(k0, kb_size), :]
            v = v_ref[pl.ds(k0, kb_size), :]
            s = lax.dot_general(q, k, (((1,), (1,)), ((), ())), preferred_element_type=jnp.float32) * scale
            key_pos = k0 + col_iota
            key_doc = kdoc_ref[:, pl.ds(k0, kb_size)]
            visible = (key_doc == row_doc) & (key_pos <= row_pos)
            s = jnp.where(visible, s, -jnp.inf)
            dp = lax.dot_general(g, v, (((1,), (1,)), ((), ())), preferred_element_type=jnp.float32)
            return k0, k, s, dp

        def first_pass(kb, c):
            @pl.when(seen(kb))
            def _():
                _, _, s, dp = scores_of(kb)
                top = top_ref[...]
                new_top = jnp.maximum(top, jnp.max(s, axis=1, keepdims=True))
                expo = jnp.exp(s - new_top)
                shrink = jnp.exp(top - new_top)
                total_ref[...] = total_ref[...] * shrink + jnp.sum(expo, axis=1, keepdims=True)
                weighted_ref[...] = weighted_ref[...] * shrink + jnp.sum(expo * dp, axis=1, keepdims=True)
                top_ref[...] = new_top
            return c

        lax.fori_loop(0, key_blocks, first_pass, 0)
        top = top_ref[...]
        total = total_ref[...]
        delta = weighted_ref[...] / total
        inverse_total = 1.0 / total

        def second_pass(kb, c):
            @pl.when(seen(kb))
            def _():
                k0, k, s, dp = scores_of(kb)
                probs = jnp.exp(s - top) * inverse_total
                probs_low = probs.astype(jnp.bfloat16)
                dscore = (probs * (dp - delta) * scale).astype(jnp.bfloat16)
                dv = lax.dot_general(probs_low, g, (((0,), (0,)), ((), ())), preferred_element_type=jnp.float32)
                dk = lax.dot_general(dscore, q, (((0,), (0,)), ((), ())), preferred_element_type=jnp.float32)
                dkv_ref[pl.ds(k0, kb_size), pl.ds(0, head_width)] += dk
                dkv_ref[pl.ds(k0, kb_size), pl.ds(head_width, head_width)] += dv
                dq_acc[...] += jnp.dot(dscore, k, preferred_element_type=jnp.float32)
            return c

        lax.fori_loop(0, key_blocks, second_pass, 0)
        dq_ref[pl.ds(r0, rb_size), :] = dq_acc[...].astype(dq_ref.dtype)
        return carry

    lax.fori_loop(0, row_blocks, row_block, 0)


def attend_kernel(flat_query, flat_grad, key_full, value_full, ends, block_start, heads, kb_size=512):
    rows, head_width = flat_query.shape
    keys = key_full.shape[0]
    rb_size = rows // block_start.shape[0]
    vmem = pltpu.VMEM
    smem = pl.BlockSpec(memory_space=pltpu.SMEM)
    whole = pl.BlockSpec(memory_space=pltpu.VMEM)
    flops = 2 * rows * keys * head_width * 7
    positions = jnp.arange(keys, dtype=jnp.int32)
    key_doc = jnp.sum((positions[:, None] >= ends[None, :]).astype(jnp.int32), axis=1)[None, :]
    return pl.pallas_call(
        functools.partial(_attend_kernel, heads, kb_size),
        out_shape=(
            jax.ShapeDtypeStruct((rows, head_width), jnp.bfloat16),
            jax.ShapeDtypeStruct((keys, 2 * head_width), jnp.float32),
        ),
        in_specs=[smem, smem, whole, whole, whole, whole, whole],
        out_specs=(whole, whole),
        scratch_shapes=[
            vmem((rb_size, 1), jnp.float32),
            vmem((rb_size, 1), jnp.float32),
            vmem((rb_size, 1), jnp.float32),
            vmem((rb_size, head_width), jnp.float32),
        ],
        compiler_params=pltpu.CompilerParams(vmem_limit_bytes=48 * 1024 * 1024),
        cost_estimate=pl.CostEstimate(flops=flops // 4, transcendentals=rows * keys // 2, bytes_accessed=rows * head_width * 6 + keys * head_width * 4 + keys * head_width * 8),
    )(ends, block_start, key_doc, flat_query, flat_grad, key_full, value_full)


def body(query, key, value, out_grad, lengths, plan):
    tokens = query.shape[1]
    width = query.shape[2]
    head_width = key.shape[2]
    shards = lax.axis_size("cp")
    own_index = lax.axis_index("cp")
    block_rows = tokens // shards
    key_count = shards * tokens
    iota = jnp.arange(shards, dtype=jnp.int32)
    inverse = jnp.sum(
        (plan[:, None, :] == iota[None, :, None]).astype(jnp.int32) * iota[None, None, :], axis=2
    )
    send_order = lax.dynamic_index_in_dim(inverse, own_index, 0, keepdims=False)

    def reorder(rows):
        grouped = rows.reshape(shards, block_rows, rows.shape[1])
        return jnp.take(grouped, send_order, axis=0)

    key_rows = tokens * head_width // width
    own_keys = jnp.concatenate([key[0].reshape(key_rows, width), value[0].reshape(key_rows, width)], axis=0)
    packed = jnp.concatenate(
        [
            reorder(query[0]),
            reorder(out_grad[0]),
            jnp.broadcast_to(own_keys[None], (shards,) + own_keys.shape),
        ],
        axis=1,
    )
    received = lax.all_to_all(packed, "cp", split_axis=0, concat_axis=0, tiled=True)
    query_sent = received[:, :block_rows]
    grad_sent = received[:, block_rows : 2 * block_rows]
    key_at = 2 * block_rows
    key_full = received[:, key_at : key_at + key_rows].reshape(key_count, head_width)
    value_full = received[:, key_at + key_rows :].reshape(key_count, head_width)
    ends = jnp.cumsum(lengths).astype(jnp.int32)
    taken = lax.dynamic_index_in_dim(inverse, own_index, 1, keepdims=False)
    head_count = width // head_width
    dquery, terms = attend_kernel(
        query_sent.reshape(tokens * head_count, head_width),
        grad_sent.reshape(tokens * head_count, head_width),
        key_full,
        value_full,
        ends,
        iota * tokens + taken * block_rows,
        head_count,
    )
    dquery = dquery.reshape(tokens, width)
    handed = passed_along(dquery, "pp", -1)
    partials = lax.all_to_all(
        terms.reshape(shards, tokens, 2 * head_width), "cp", split_axis=0, concat_axis=0, tiled=True
    )
    summed = jnp.sum(partials, axis=0)
    key_grad = summed[:, :head_width].astype(jnp.bfloat16)
    value_grad = summed[:, head_width:].astype(jnp.bfloat16)
    return (handed[None], key_grad[None], value_grad[None])


def solution(mesh):
    return jax.shard_map(
        body,
        mesh=mesh,
        in_specs=(
            P("pp", "cp", "tp"),
            P("pp", "cp", "tp"),
            P("pp", "cp", "tp"),
            P("pp", "cp", "tp"),
            P(),
            P(),
        ),
        out_specs=(P("pp", "cp", "tp"), P("pp", "cp", "tp"), P("pp", "cp", "tp")),
        check_vma=False,
    )
```

```python
import functools

import jax
import jax.numpy as jnp
from jax import lax
from jax.sharding import PartitionSpec as P
from jax.experimental import pallas as pl
from jax.experimental.pallas import tpu as pltpu


def passed_along(array, axis, by):
    peers = lax.axis_size(axis)
    pairs = [(i, i + by) for i in range(peers) if 0 <= i + by < peers]
    return lax.ppermute(array, axis, pairs)


def _doc_of(ends_ref, position):
    doc = jnp.int32(0)
    for i in range(ends_ref.shape[0]):
        doc = doc + (position >= ends_ref[i]).astype(jnp.int32)
    return doc


def _attend_kernel(heads, kb_size, ends_ref, start_ref, kdoc_ref, q_ref, g_ref, k_ref, v_ref, dq_ref, dkv_ref, top_ref, total_ref, weighted_ref, dq_acc):
    rows, head_width = q_ref.shape
    keys = k_ref.shape[0]
    rb_size = rows // start_ref.shape[0]
    row_blocks = rows // rb_size
    key_blocks = keys // kb_size
    tokens_per_block = rb_size // heads
    scale = head_width ** (-0.5)
    dkv_ref[...] = jnp.zeros_like(dkv_ref)
    row_iota = lax.broadcasted_iota(jnp.int32, (rb_size, kb_size), 0) // heads
    col_iota = lax.broadcasted_iota(jnp.int32, (rb_size, kb_size), 1)
    row_iota1 = lax.broadcasted_iota(jnp.int32, (rb_size, 1), 0) // heads

    def vector_doc(position):
        doc = jnp.zeros(position.shape, jnp.int32)
        for i in range(ends_ref.shape[0]):
            doc = doc + (position >= ends_ref[i]).astype(jnp.int32)
        return doc

    def row_block(rb, carry):
        first = start_ref[rb]
        last = first + tokens_per_block - 1
        first_doc = _doc_of(ends_ref, first)
        last_doc = _doc_of(ends_ref, last)
        r0 = pl.multiple_of(rb * rb_size, rb_size)
        q = q_ref[pl.ds(r0, rb_size), :]
        g = g_ref[pl.ds(r0, rb_size), :]
        row_pos = first + row_iota
        row_doc = vector_doc(first + row_iota1)
        top_ref[...] = jnp.full(top_ref.shape, -1e30, jnp.float32)
        total_ref[...] = jnp.zeros(total_ref.shape, jnp.float32)
        weighted_ref[...] = jnp.zeros(weighted_ref.shape, jnp.float32)
        dq_acc[...] = jnp.zeros(dq_acc.shape, jnp.float32)

        def seen(kb):
            k0 = kb * kb_size
            return (k0 <= last) & (_doc_of(ends_ref, k0) <= last_doc) & (_doc_of(ends_ref, k0 + kb_size - 1) >= first_doc)

        def scores_of(kb):
            k0 = pl.multiple_of(kb * kb_size, kb_size)
            k = k_ref[pl.ds(k0, kb_size), :]
            v = v_ref[pl.ds(k0, kb_size), :]
            s = lax.dot_general(q, k, (((1,), (1,)), ((), ())), preferred_element_type=jnp.float32) * scale
            key_pos = k0 + col_iota
            key_doc = kdoc_ref[:, pl.ds(k0, kb_size)]
            visible = (key_doc == row_doc) & (key_pos <= row_pos)
            s = jnp.where(visible, s, -jnp.inf)
            dp = lax.dot_general(g, v, (((1,), (1,)), ((), ())), preferred_element_type=jnp.float32)
            return k0, k, s, dp

        def first_pass(kb, c):
            @pl.when(seen(kb))
            def _():
                _, _, s, dp = scores_of(kb)
                top = top_ref[...]
                new_top = jnp.maximum(top, jnp.max(s, axis=1, keepdims=True))
                expo = jnp.exp(s - new_top)
                shrink = jnp.exp(top - new_top)
                total_ref[...] = total_ref[...] * shrink + jnp.sum(expo, axis=1, keepdims=True)
                weighted_ref[...] = weighted_ref[...] * shrink + jnp.sum(expo * dp, axis=1, keepdims=True)
                top_ref[...] = new_top
            return c

        lax.fori_loop(0, key_blocks, first_pass, 0)
        top = top_ref[...]
        total = total_ref[...]
        delta = weighted_ref[...] / total
        inverse_total = 1.0 / total

        def second_pass(kb, c):
            @pl.when(seen(kb))
            def _():
                k0, k, s, dp = scores_of(kb)
                probs = jnp.exp(s - top) * inverse_total
                probs_low = probs.astype(jnp.bfloat16)
                dscore = (probs * (dp - delta) * scale).astype(jnp.bfloat16)
                dv = lax.dot_general(probs_low, g, (((0,), (0,)), ((), ())), preferred_element_type=jnp.float32)
                dk = lax.dot_general(dscore, q, (((0,), (0,)), ((), ())), preferred_element_type=jnp.float32)
                dkv_ref[pl.ds(k0, kb_size), pl.ds(0, head_width)] += dk
                dkv_ref[pl.ds(k0, kb_size), pl.ds(head_width, head_width)] += dv
                dq_acc[...] += jnp.dot(dscore, k, preferred_element_type=jnp.float32)
            return c

        lax.fori_loop(0, key_blocks, second_pass, 0)
        dq_ref[pl.ds(r0, rb_size), :] = dq_acc[...].astype(dq_ref.dtype)
        return carry

    lax.fori_loop(0, row_blocks, row_block, 0)


def attend_kernel(flat_query, flat_grad, key_full, value_full, ends, block_start, heads, kb_size=512):
    rows, head_width = flat_query.shape
    keys = key_full.shape[0]
    rb_size = rows // block_start.shape[0]
    vmem = pltpu.VMEM
    smem = pl.BlockSpec(memory_space=pltpu.SMEM)
    whole = pl.BlockSpec(memory_space=pltpu.VMEM)
    flops = 2 * rows * keys * head_width * 7
    positions = jnp.arange(keys, dtype=jnp.int32)
    key_doc = jnp.sum((positions[:, None] >= ends[None, :]).astype(jnp.int32), axis=1)[None, :]
    return pl.pallas_call(
        functools.partial(_attend_kernel, heads, kb_size),
        out_shape=(
            jax.ShapeDtypeStruct((rows, head_width), jnp.bfloat16),
            jax.ShapeDtypeStruct((keys, 2 * head_width), jnp.float32),
        ),
        in_specs=[smem, smem, whole, whole, whole, whole, whole],
        out_specs=(whole, whole),
        scratch_shapes=[
            vmem((rb_size, 1), jnp.float32),
            vmem((rb_size, 1), jnp.float32),
            vmem((rb_size, 1), jnp.float32),
            vmem((rb_size, head_width), jnp.float32),
        ],
        compiler_params=pltpu.CompilerParams(vmem_limit_bytes=48 * 1024 * 1024),
        cost_estimate=pl.CostEstimate(flops=flops // 4, transcendentals=rows * keys // 2, bytes_accessed=rows * head_width * 6 + keys * head_width * 4 + keys * head_width * 8),
    )(ends, block_start, key_doc, flat_query, flat_grad, key_full, value_full)


def body(query, key, value, out_grad, lengths, plan):
    tokens = query.shape[1]
    width = query.shape[2]
    head_width = key.shape[2]
    shards = lax.axis_size("cp")
    own_index = lax.axis_index("cp")
    block_rows = tokens // shards
    key_count = shards * tokens
    iota = jnp.arange(shards, dtype=jnp.int32)
    inverse = jnp.sum(
        (plan[:, None, :] == iota[None, :, None]).astype(jnp.int32) * iota[None, None, :], axis=2
    )
    send_order = lax.dynamic_index_in_dim(inverse, own_index, 0, keepdims=False)

    def reorder(rows):
        grouped = rows.reshape(shards, block_rows, rows.shape[1])
        return jnp.take(grouped, send_order, axis=0)

    key_rows = tokens * head_width // width
    own_keys = jnp.concatenate([key[0].reshape(key_rows, width), value[0].reshape(key_rows, width)], axis=0)
    packed = jnp.concatenate(
        [
            reorder(query[0]),
            reorder(out_grad[0]),
            jnp.broadcast_to(own_keys[None], (shards,) + own_keys.shape),
        ],
        axis=1,
    )
    received = lax.all_to_all(packed, "cp", split_axis=0, concat_axis=0, tiled=True)
    query_sent = received[:, :block_rows]
    grad_sent = received[:, block_rows : 2 * block_rows]
    key_at = 2 * block_rows
    key_full = received[:, key_at : key_at + key_rows].reshape(key_count, head_width)
    value_full = received[:, key_at + key_rows :].reshape(key_count, head_width)
    ends = jnp.cumsum(lengths).astype(jnp.int32)
    taken = lax.dynamic_index_in_dim(inverse, own_index, 1, keepdims=False)
    head_count = width // head_width
    dquery, terms = attend_kernel(
        query_sent.reshape(tokens * head_count, head_width),
        grad_sent.reshape(tokens * head_count, head_width),
        key_full,
        value_full,
        ends,
        iota * tokens + taken * block_rows,
        head_count,
    )
    dquery = dquery.reshape(tokens, width)
    handed = passed_along(dquery, "pp", -1)
    partials = lax.all_to_all(
        terms.astype(jnp.bfloat16).reshape(shards, tokens, 2 * head_width), "cp", split_axis=0, concat_axis=0, tiled=True
    )
    summed = jnp.sum(partials.astype(jnp.float32), axis=0)
    key_grad = summed[:, :head_width].astype(jnp.bfloat16)
    value_grad = summed[:, head_width:].astype(jnp.bfloat16)
    return (handed[None], key_grad[None], value_grad[None])


def solution(mesh):
    return jax.shard_map(
        body,
        mesh=mesh,
        in_specs=(
            P("pp", "cp", "tp"),
            P("pp", "cp", "tp"),
            P("pp", "cp", "tp"),
            P("pp", "cp", "tp"),
            P(),
            P(),
        ),
        out_specs=(P("pp", "cp", "tp"), P("pp", "cp", "tp"), P("pp", "cp", "tp")),
        check_vma=False,
    )
```

```python
import functools

import jax
import jax.numpy as jnp
from jax import lax
from jax.sharding import PartitionSpec as P
from jax.experimental import pallas as pl
from jax.experimental.pallas import tpu as pltpu


def passed_along(array, axis, by):
    peers = lax.axis_size(axis)
    pairs = [(i, i + by) for i in range(peers) if 0 <= i + by < peers]
    return lax.ppermute(array, axis, pairs)


def _doc_of(ends_ref, position):
    doc = jnp.int32(0)
    for i in range(ends_ref.shape[0]):
        doc = doc + (position >= ends_ref[i]).astype(jnp.int32)
    return doc


def _attend_kernel(heads, kb_size, ends_ref, start_ref, kdoc_ref, q_ref, g_ref, kv_ref, dq_ref, dkv_ref, top_ref, total_ref, weighted_ref, dq_acc):
    rows, head_width = q_ref.shape
    keys = kv_ref.shape[0]
    rb_size = rows // start_ref.shape[0]
    row_blocks = rows // rb_size
    key_blocks = keys // kb_size
    tokens_per_block = rb_size // heads
    scale = head_width ** (-0.5)
    dkv_ref[...] = jnp.zeros_like(dkv_ref)
    row_iota = lax.broadcasted_iota(jnp.int32, (rb_size, kb_size), 0) // heads
    col_iota = lax.broadcasted_iota(jnp.int32, (rb_size, kb_size), 1)
    row_iota1 = lax.broadcasted_iota(jnp.int32, (rb_size, 1), 0) // heads

    def vector_doc(position):
        doc = jnp.zeros(position.shape, jnp.int32)
        for i in range(ends_ref.shape[0]):
            doc = doc + (position >= ends_ref[i]).astype(jnp.int32)
        return doc

    def row_block(rb, carry):
        first = start_ref[rb]
        last = first + tokens_per_block - 1
        first_doc = _doc_of(ends_ref, first)
        last_doc = _doc_of(ends_ref, last)
        r0 = pl.multiple_of(rb * rb_size, rb_size)
        q = q_ref[pl.ds(r0, rb_size), :]
        g = g_ref[pl.ds(r0, rb_size), :]
        row_pos = first + row_iota
        row_doc = vector_doc(first + row_iota1)
        top_ref[...] = jnp.full(top_ref.shape, -1e30, jnp.float32)
        total_ref[...] = jnp.zeros(total_ref.shape, jnp.float32)
        weighted_ref[...] = jnp.zeros(weighted_ref.shape, jnp.float32)
        dq_acc[...] = jnp.zeros(dq_acc.shape, jnp.float32)

        def seen(kb):
            k0 = kb * kb_size
            return (k0 <= last) & (_doc_of(ends_ref, k0) <= last_doc) & (_doc_of(ends_ref, k0 + kb_size - 1) >= first_doc)

        def scores_of(kb):
            k0 = pl.multiple_of(kb * kb_size, kb_size)
            k = kv_ref[pl.ds(k0, kb_size), pl.ds(0, head_width)]
            v = kv_ref[pl.ds(k0, kb_size), pl.ds(head_width, head_width)]
            s = lax.dot_general(q, k, (((1,), (1,)), ((), ())), preferred_element_type=jnp.float32) * scale
            key_pos = k0 + col_iota
            key_doc = kdoc_ref[:, pl.ds(k0, kb_size)]
            visible = (key_doc == row_doc) & (key_pos <= row_pos)
            s = jnp.where(visible, s, -jnp.inf)
            dp = lax.dot_general(g, v, (((1,), (1,)), ((), ())), preferred_element_type=jnp.float32)
            return k0, k, s, dp

        def first_pass(kb, c):
            @pl.when(seen(kb))
            def _():
                _, _, s, dp = scores_of(kb)
                top = top_ref[...]
                new_top = jnp.maximum(top, jnp.max(s, axis=1, keepdims=True))
                expo = jnp.exp(s - new_top)
                shrink = jnp.exp(top - new_top)
                total_ref[...] = total_ref[...] * shrink + jnp.sum(expo, axis=1, keepdims=True)
                weighted_ref[...] = weighted_ref[...] * shrink + jnp.sum(expo * dp, axis=1, keepdims=True)
                top_ref[...] = new_top
            return c

        lax.fori_loop(0, key_blocks, first_pass, 0)
        top = top_ref[...]
        total = total_ref[...]
        delta = weighted_ref[...] / total
        inverse_total = 1.0 / total

        def second_pass(kb, c):
            @pl.when(seen(kb))
            def _():
                k0, k, s, dp = scores_of(kb)
                probs = jnp.exp(s - top) * inverse_total
                probs_low = probs.astype(jnp.bfloat16)
                dscore = (probs * (dp - delta) * scale).astype(jnp.bfloat16)
                dv = lax.dot_general(probs_low, g, (((0,), (0,)), ((), ())), preferred_element_type=jnp.float32)
                dk = lax.dot_general(dscore, q, (((0,), (0,)), ((), ())), preferred_element_type=jnp.float32)
                dkv_ref[pl.ds(k0, kb_size), pl.ds(0, head_width)] += dk
                dkv_ref[pl.ds(k0, kb_size), pl.ds(head_width, head_width)] += dv
                dq_acc[...] += jnp.dot(dscore, k, preferred_element_type=jnp.float32)
            return c

        lax.fori_loop(0, key_blocks, second_pass, 0)
        dq_ref[pl.ds(r0, rb_size), :] = dq_acc[...].astype(dq_ref.dtype)
        return carry

    lax.fori_loop(0, row_blocks, row_block, 0)


def attend_kernel(flat_query, flat_grad, keys_all, ends, block_start, heads, kb_size=512):
    rows, head_width = flat_query.shape
    keys = keys_all.shape[0]
    rb_size = rows // block_start.shape[0]
    vmem = pltpu.VMEM
    smem = pl.BlockSpec(memory_space=pltpu.SMEM)
    whole = pl.BlockSpec(memory_space=pltpu.VMEM)
    flops = 2 * rows * keys * head_width * 7
    positions = jnp.arange(keys, dtype=jnp.int32)
    key_doc = jnp.sum((positions[:, None] >= ends[None, :]).astype(jnp.int32), axis=1)[None, :]
    return pl.pallas_call(
        functools.partial(_attend_kernel, heads, kb_size),
        out_shape=(
            jax.ShapeDtypeStruct((rows, head_width), jnp.bfloat16),
            jax.ShapeDtypeStruct((keys, 2 * head_width), jnp.float32),
        ),
        in_specs=[smem, smem, whole, whole, whole, whole],
        out_specs=(whole, whole),
        scratch_shapes=[
            vmem((rb_size, 1), jnp.float32),
            vmem((rb_size, 1), jnp.float32),
            vmem((rb_size, 1), jnp.float32),
            vmem((rb_size, head_width), jnp.float32),
        ],
        compiler_params=pltpu.CompilerParams(vmem_limit_bytes=48 * 1024 * 1024),
        cost_estimate=pl.CostEstimate(flops=flops // 4, transcendentals=rows * keys // 2, bytes_accessed=rows * head_width * 6 + keys * head_width * 4 + keys * head_width * 8),
    )(ends, block_start, key_doc, flat_query, flat_grad, keys_all)


def body(query, key, value, out_grad, lengths, plan):
    tokens = query.shape[1]
    width = query.shape[2]
    head_width = key.shape[2]
    shards = lax.axis_size("cp")
    own_index = lax.axis_index("cp")
    block_rows = tokens // shards
    key_count = shards * tokens
    iota = jnp.arange(shards, dtype=jnp.int32)
    inverse = jnp.sum(
        (plan[:, None, :] == iota[None, :, None]).astype(jnp.int32) * iota[None, None, :], axis=2
    )
    send_order = lax.dynamic_index_in_dim(inverse, own_index, 0, keepdims=False)

    def reorder(rows):
        grouped = rows.reshape(shards, block_rows, rows.shape[1])
        return jnp.take(grouped, send_order, axis=0)

    rows_sent = jnp.concatenate([reorder(query[0]), reorder(out_grad[0])], axis=1)
    received = lax.all_to_all(rows_sent, "cp", split_axis=0, concat_axis=0, tiled=True)
    query_sent = received[:, :block_rows]
    grad_sent = received[:, block_rows:]
    held = jnp.concatenate([key[0], value[0]], axis=1)[None]
    step = 1
    while step < shards:
        pairs = [(i, i ^ step) for i in range(shards)]
        other = lax.ppermute(held, "cp", pairs)
        upper = (own_index & step) != 0
        held = jnp.where(upper, jnp.concatenate([other, held], 0), jnp.concatenate([held, other], 0))
        step *= 2
    keys_all = held.reshape(key_count, 2 * head_width)
    ends = jnp.cumsum(lengths).astype(jnp.int32)
    taken = lax.dynamic_index_in_dim(inverse, own_index, 1, keepdims=False)
    head_count = width // head_width
    dquery, terms = attend_kernel(
        query_sent.reshape(tokens * head_count, head_width),
        grad_sent.reshape(tokens * head_count, head_width),
        keys_all,
        ends,
        iota * tokens + taken * block_rows,
        head_count,
    )
    dquery = dquery.reshape(tokens, width)
    handed = passed_along(dquery, "pp", -1)
    partials = lax.all_to_all(
        terms.astype(jnp.bfloat16).reshape(shards, tokens, 2 * head_width), "cp", split_axis=0, concat_axis=0, tiled=True
    )
    summed = jnp.sum(partials.astype(jnp.float32), axis=0)
    key_grad = summed[:, :head_width].astype(jnp.bfloat16)
    value_grad = summed[:, head_width:].astype(jnp.bfloat16)
    return (handed[None], key_grad[None], value_grad[None])


def solution(mesh):
    return jax.shard_map(
        body,
        mesh=mesh,
        in_specs=(
            P("pp", "cp", "tp"),
            P("pp", "cp", "tp"),
            P("pp", "cp", "tp"),
            P("pp", "cp", "tp"),
            P(),
            P(),
        ),
        out_specs=(P("pp", "cp", "tp"), P("pp", "cp", "tp"), P("pp", "cp", "tp")),
        check_vma=False,
    )
```

```python
import functools

import jax
import jax.numpy as jnp
from jax import lax
from jax.sharding import PartitionSpec as P
from jax.experimental import pallas as pl
from jax.experimental.pallas import tpu as pltpu


def passed_along(array, axis, by):
    peers = lax.axis_size(axis)
    pairs = [(i, i + by) for i in range(peers) if 0 <= i + by < peers]
    return lax.ppermute(array, axis, pairs)


def _doc_of(ends_ref, position):
    doc = jnp.int32(0)
    for i in range(ends_ref.shape[0]):
        doc = doc + (position >= ends_ref[i]).astype(jnp.int32)
    return doc


def _attend_kernel(heads, kb_size, ends_ref, start_ref, kdoc_ref, q_ref, g_ref, k_ref, v_ref, dq_ref, dkv_ref, top_ref, total_ref, weighted_ref, dq_acc):
    rows, head_width = q_ref.shape
    keys = k_ref.shape[0]
    rb_size = rows // start_ref.shape[0]
    row_blocks = rows // rb_size
    key_blocks = keys // kb_size
    tokens_per_block = rb_size // heads
    scale = head_width ** (-0.5)
    dkv_ref[...] = jnp.zeros_like(dkv_ref)
    row_iota = lax.broadcasted_iota(jnp.int32, (rb_size, kb_size), 0) // heads
    col_iota = lax.broadcasted_iota(jnp.int32, (rb_size, kb_size), 1)
    row_iota1 = lax.broadcasted_iota(jnp.int32, (rb_size, 1), 0) // heads

    def vector_doc(position):
        doc = jnp.zeros(position.shape, jnp.int32)
        for i in range(ends_ref.shape[0]):
            doc = doc + (position >= ends_ref[i]).astype(jnp.int32)
        return doc

    def row_block(rb, carry):
        first = start_ref[rb]
        last = first + tokens_per_block - 1
        first_doc = _doc_of(ends_ref, first)
        last_doc = _doc_of(ends_ref, last)
        r0 = pl.multiple_of(rb * rb_size, rb_size)
        q = q_ref[pl.ds(r0, rb_size), :]
        g = g_ref[pl.ds(r0, rb_size), :]
        row_pos = first + row_iota
        row_doc = vector_doc(first + row_iota1)
        top_ref[...] = jnp.full(top_ref.shape, -1e30, jnp.float32)
        total_ref[...] = jnp.zeros(total_ref.shape, jnp.float32)
        weighted_ref[...] = jnp.zeros(weighted_ref.shape, jnp.float32)
        dq_acc[...] = jnp.zeros(dq_acc.shape, jnp.float32)

        def seen(kb):
            k0 = kb * kb_size
            return (k0 <= last) & (_doc_of(ends_ref, k0) <= last_doc) & (_doc_of(ends_ref, k0 + kb_size - 1) >= first_doc)

        def scores_of(kb):
            k0 = pl.multiple_of(kb * kb_size, kb_size)
            k = k_ref[pl.ds(k0, kb_size), :]
            v = v_ref[pl.ds(k0, kb_size), :]
            s = lax.dot_general(q, k, (((1,), (1,)), ((), ())), preferred_element_type=jnp.float32) * scale
            key_pos = k0 + col_iota
            key_doc = kdoc_ref[:, pl.ds(k0, kb_size)]
            visible = (key_doc == row_doc) & (key_pos <= row_pos)
            s = jnp.where(visible, s, -jnp.inf)
            dp = lax.dot_general(g, v, (((1,), (1,)), ((), ())), preferred_element_type=jnp.float32)
            return k0, k, s, dp

        def first_pass(kb, c):
            @pl.when(seen(kb))
            def _():
                _, _, s, dp = scores_of(kb)
                top = top_ref[...]
                new_top = jnp.maximum(top, jnp.max(s, axis=1, keepdims=True))
                expo = jnp.exp(s - new_top)
                shrink = jnp.exp(top - new_top)
                total_ref[...] = total_ref[...] * shrink + jnp.sum(expo, axis=1, keepdims=True)
                weighted_ref[...] = weighted_ref[...] * shrink + jnp.sum(expo * dp, axis=1, keepdims=True)
                top_ref[...] = new_top
            return c

        lax.fori_loop(0, key_blocks, first_pass, 0)
        top = top_ref[...]
        total = total_ref[...]
        delta = weighted_ref[...] / total
        inverse_total = 1.0 / total

        def second_pass(kb, c):
            @pl.when(seen(kb))
            def _():
                k0, k, s, dp = scores_of(kb)
                probs = jnp.exp(s - top) * inverse_total
                probs_low = probs.astype(jnp.bfloat16)
                dscore = (probs * (dp - delta) * scale).astype(jnp.bfloat16)
                dv = lax.dot_general(probs_low, g, (((0,), (0,)), ((), ())), preferred_element_type=jnp.float32)
                dk = lax.dot_general(dscore, q, (((0,), (0,)), ((), ())), preferred_element_type=jnp.float32)
                dkv_ref[pl.ds(k0, kb_size), pl.ds(0, head_width)] += dk
                dkv_ref[pl.ds(k0, kb_size), pl.ds(head_width, head_width)] += dv
                dq_acc[...] += jnp.dot(dscore, k, preferred_element_type=jnp.float32)
            return c

        lax.fori_loop(0, key_blocks, second_pass, 0)
        dq_ref[pl.ds(r0, rb_size), :] = dq_acc[...].astype(dq_ref.dtype)
        return carry

    lax.fori_loop(0, row_blocks, row_block, 0)


def attend_kernel(flat_query, flat_grad, key_full, value_full, ends, block_start, heads, kb_size=1024):
    rows, head_width = flat_query.shape
    keys = key_full.shape[0]
    rb_size = rows // block_start.shape[0]
    vmem = pltpu.VMEM
    smem = pl.BlockSpec(memory_space=pltpu.SMEM)
    whole = pl.BlockSpec(memory_space=pltpu.VMEM)
    flops = 2 * rows * keys * head_width * 7
    positions = jnp.arange(keys, dtype=jnp.int32)
    key_doc = jnp.sum((positions[:, None] >= ends[None, :]).astype(jnp.int32), axis=1)[None, :]
    return pl.pallas_call(
        functools.partial(_attend_kernel, heads, kb_size),
        out_shape=(
            jax.ShapeDtypeStruct((rows, head_width), jnp.bfloat16),
            jax.ShapeDtypeStruct((keys, 2 * head_width), jnp.float32),
        ),
        in_specs=[smem, smem, whole, whole, whole, whole, whole],
        out_specs=(whole, whole),
        scratch_shapes=[
            vmem((rb_size, 1), jnp.float32),
            vmem((rb_size, 1), jnp.float32),
            vmem((rb_size, 1), jnp.float32),
            vmem((rb_size, head_width), jnp.float32),
        ],
        compiler_params=pltpu.CompilerParams(vmem_limit_bytes=48 * 1024 * 1024),
        cost_estimate=pl.CostEstimate(flops=flops // 4, transcendentals=rows * keys // 2, bytes_accessed=rows * head_width * 6 + keys * head_width * 4 + keys * head_width * 8),
    )(ends, block_start, key_doc, flat_query, flat_grad, key_full, value_full)


def body(query, key, value, out_grad, lengths, plan):
    tokens = query.shape[1]
    width = query.shape[2]
    head_width = key.shape[2]
    shards = lax.axis_size("cp")
    own_index = lax.axis_index("cp")
    block_rows = tokens // shards
    key_count = shards * tokens
    iota = jnp.arange(shards, dtype=jnp.int32)
    inverse = jnp.sum(
        (plan[:, None, :] == iota[None, :, None]).astype(jnp.int32) * iota[None, None, :], axis=2
    )
    send_order = lax.dynamic_index_in_dim(inverse, own_index, 0, keepdims=False)

    def reorder(rows):
        grouped = rows.reshape(shards, block_rows, rows.shape[1])
        return jnp.take(grouped, send_order, axis=0)

    key_rows = tokens * head_width // width
    own_keys = jnp.concatenate([key[0].reshape(key_rows, width), value[0].reshape(key_rows, width)], axis=0)
    packed = jnp.concatenate(
        [
            reorder(query[0]),
            reorder(out_grad[0]),
            jnp.broadcast_to(own_keys[None], (shards,) + own_keys.shape),
        ],
        axis=1,
    )
    received = lax.all_to_all(packed, "cp", split_axis=0, concat_axis=0, tiled=True)
    query_sent = received[:, :block_rows]
    grad_sent = received[:, block_rows : 2 * block_rows]
    key_at = 2 * block_rows
    key_full = received[:, key_at : key_at + key_rows].reshape(key_count, head_width)
    value_full = received[:, key_at + key_rows :].reshape(key_count, head_width)
    ends = jnp.cumsum(lengths).astype(jnp.int32)
    taken = lax.dynamic_index_in_dim(inverse, own_index, 1, keepdims=False)
    head_count = width // head_width
    dquery, terms = attend_kernel(
        query_sent.reshape(tokens * head_count, head_width),
        grad_sent.reshape(tokens * head_count, head_width),
        key_full,
        value_full,
        ends,
        iota * tokens + taken * block_rows,
        head_count,
    )
    dquery = dquery.reshape(tokens, width)
    handed = passed_along(dquery, "pp", -1)
    partials = lax.all_to_all(
        terms.astype(jnp.bfloat16).reshape(shards, tokens, 2 * head_width), "cp", split_axis=0, concat_axis=0, tiled=True
    )
    summed = jnp.sum(partials.astype(jnp.float32), axis=0)
    key_grad = summed[:, :head_width].astype(jnp.bfloat16)
    value_grad = summed[:, head_width:].astype(jnp.bfloat16)
    return (handed[None], key_grad[None], value_grad[None])


def solution(mesh):
    return jax.shard_map(
        body,
        mesh=mesh,
        in_specs=(
            P("pp", "cp", "tp"),
            P("pp", "cp", "tp"),
            P("pp", "cp", "tp"),
            P("pp", "cp", "tp"),
            P(),
            P(),
        ),
        out_specs=(P("pp", "cp", "tp"), P("pp", "cp", "tp"), P("pp", "cp", "tp")),
        check_vma=False,
    )
```

```python
import functools

import jax
import jax.numpy as jnp
from jax import lax
from jax.sharding import PartitionSpec as P
from jax.experimental import pallas as pl
from jax.experimental.pallas import tpu as pltpu


def passed_along(array, axis, by):
    peers = lax.axis_size(axis)
    pairs = [(i, i + by) for i in range(peers) if 0 <= i + by < peers]
    return lax.ppermute(array, axis, pairs)


def _doc_of(ends_ref, position):
    doc = jnp.int32(0)
    for i in range(ends_ref.shape[0]):
        doc = doc + (position >= ends_ref[i]).astype(jnp.int32)
    return doc


def _attend_kernel(heads, kb_size, ends_ref, start_ref, kdoc_ref, q_ref, g_ref, k_ref, v_ref, dq_ref, dkv_ref, top_ref, total_ref, weighted_ref, dq_acc):
    rows, head_width = q_ref.shape
    keys = k_ref.shape[0]
    rb_size = rows // start_ref.shape[0]
    row_blocks = rows // rb_size
    key_blocks = keys // kb_size
    tokens_per_block = rb_size // heads
    scale = head_width ** (-0.5)
    dkv_ref[...] = jnp.zeros_like(dkv_ref)
    row_iota = lax.broadcasted_iota(jnp.int32, (rb_size, kb_size), 0) // heads
    col_iota = lax.broadcasted_iota(jnp.int32, (rb_size, kb_size), 1)
    row_iota1 = lax.broadcasted_iota(jnp.int32, (rb_size, 1), 0) // heads

    def vector_doc(position):
        doc = jnp.zeros(position.shape, jnp.int32)
        for i in range(ends_ref.shape[0]):
            doc = doc + (position >= ends_ref[i]).astype(jnp.int32)
        return doc

    def row_block(rb, carry):
        first = start_ref[rb]
        last = first + tokens_per_block - 1
        first_doc = _doc_of(ends_ref, first)
        last_doc = _doc_of(ends_ref, last)
        r0 = pl.multiple_of(rb * rb_size, rb_size)
        q = q_ref[pl.ds(r0, rb_size), :]
        g = g_ref[pl.ds(r0, rb_size), :]
        row_pos = first + row_iota
        row_doc = vector_doc(first + row_iota1)
        top_ref[...] = jnp.full(top_ref.shape, -1e30, jnp.float32)
        total_ref[...] = jnp.zeros(total_ref.shape, jnp.float32)
        weighted_ref[...] = jnp.zeros(weighted_ref.shape, jnp.float32)
        dq_acc[...] = jnp.zeros(dq_acc.shape, jnp.float32)

        def seen(kb):
            k0 = kb * kb_size
            return (k0 <= last) & (_doc_of(ends_ref, k0) <= last_doc) & (_doc_of(ends_ref, k0 + kb_size - 1) >= first_doc)

        def scores_of(kb):
            k0 = pl.multiple_of(kb * kb_size, kb_size)
            k = k_ref[pl.ds(k0, kb_size), :]
            v = v_ref[pl.ds(k0, kb_size), :]
            s = lax.dot_general(q, k, (((1,), (1,)), ((), ())), preferred_element_type=jnp.float32) * scale
            key_pos = k0 + col_iota
            key_doc = kdoc_ref[:, pl.ds(k0, kb_size)]
            visible = (key_doc == row_doc) & (key_pos <= row_pos)
            s = jnp.where(visible, s, -jnp.inf)
            dp = lax.dot_general(g, v, (((1,), (1,)), ((), ())), preferred_element_type=jnp.float32)
            return k0, k, s, dp

        def first_pass(kb, c):
            @pl.when(seen(kb))
            def _():
                _, _, s, dp = scores_of(kb)
                top = top_ref[...]
                new_top = jnp.maximum(top, jnp.max(s, axis=1, keepdims=True))
                expo = jnp.exp(s - new_top)
                shrink = jnp.exp(top - new_top)
                total_ref[...] = total_ref[...] * shrink + jnp.sum(expo, axis=1, keepdims=True)
                weighted_ref[...] = weighted_ref[...] * shrink + jnp.sum(expo * dp, axis=1, keepdims=True)
                top_ref[...] = new_top
            return c

        lax.fori_loop(0, key_blocks, first_pass, 0)
        top = top_ref[...]
        total = total_ref[...]
        delta = weighted_ref[...] / total
        inverse_total = 1.0 / total

        def second_pass(kb, c):
            @pl.when(seen(kb))
            def _():
                k0, k, s, dp = scores_of(kb)
                probs = jnp.exp(s - top) * inverse_total
                probs_low = probs.astype(jnp.bfloat16)
                dscore = (probs * (dp - delta) * scale).astype(jnp.bfloat16)
                dv = lax.dot_general(probs_low, g, (((0,), (0,)), ((), ())), preferred_element_type=jnp.float32)
                dk = lax.dot_general(dscore, q, (((0,), (0,)), ((), ())), preferred_element_type=jnp.float32)
                dkv_ref[pl.ds(k0, kb_size), pl.ds(0, head_width)] += dk
                dkv_ref[pl.ds(k0, kb_size), pl.ds(head_width, head_width)] += dv
                dq_acc[...] += jnp.dot(dscore, k, preferred_element_type=jnp.float32)
            return c

        lax.fori_loop(0, key_blocks, second_pass, 0)
        dq_ref[pl.ds(r0, rb_size), :] = dq_acc[...].astype(dq_ref.dtype)
        return carry

    lax.fori_loop(0, row_blocks, row_block, 0)


def attend_kernel(flat_query, flat_grad, key_full, value_full, ends, block_start, heads, kb_size=1024):
    rows, head_width = flat_query.shape
    keys = key_full.shape[0]
    rb_size = rows // block_start.shape[0]
    vmem = pltpu.VMEM
    smem = pl.BlockSpec(memory_space=pltpu.SMEM)
    whole = pl.BlockSpec(memory_space=pltpu.VMEM)
    flops = 2 * rows * keys * head_width * 7
    positions = jnp.arange(keys, dtype=jnp.int32)
    key_doc = jnp.sum((positions[:, None] >= ends[None, :]).astype(jnp.int32), axis=1)[None, :]
    return pl.pallas_call(
        functools.partial(_attend_kernel, heads, kb_size),
        out_shape=(
            jax.ShapeDtypeStruct((rows, head_width), jnp.bfloat16),
            jax.ShapeDtypeStruct((keys, 2 * head_width), jnp.float32),
        ),
        in_specs=[smem, smem, whole, whole, whole, whole, whole],
        out_specs=(whole, whole),
        scratch_shapes=[
            vmem((rb_size, 1), jnp.float32),
            vmem((rb_size, 1), jnp.float32),
            vmem((rb_size, 1), jnp.float32),
            vmem((rb_size, head_width), jnp.float32),
        ],
        compiler_params=pltpu.CompilerParams(vmem_limit_bytes=48 * 1024 * 1024),
        cost_estimate=pl.CostEstimate(flops=flops // 4, transcendentals=rows * keys // 2, bytes_accessed=rows * head_width * 6 + keys * head_width * 4 + keys * head_width * 8),
    )(ends, block_start, key_doc, flat_query, flat_grad, key_full, value_full)


def body(query, key, value, out_grad, lengths, plan):
    tokens = query.shape[1]
    width = query.shape[2]
    head_width = key.shape[2]
    head_count = width // head_width
    shards = lax.axis_size("cp")
    own_index = lax.axis_index("cp")
    block_rows = tokens // shards
    key_count = shards * tokens
    iota = jnp.arange(shards, dtype=jnp.int32)
    inverse = jnp.sum(
        (plan[:, None, :] == iota[None, :, None]).astype(jnp.int32) * iota[None, None, :], axis=2
    )
    send_order = lax.dynamic_index_in_dim(inverse, own_index, 0, keepdims=False)

    def reorder(rows):
        grouped = rows.reshape(shards, block_rows, rows.shape[1])
        return jnp.take(grouped, send_order, axis=0)

    key_rows = tokens * head_width // width
    own_keys = jnp.concatenate([key[0].reshape(key_rows, width), value[0].reshape(key_rows, width)], axis=0)
    keys_taken = lax.all_to_all(
        jnp.broadcast_to(own_keys[None], (shards,) + own_keys.shape), "cp", split_axis=0, concat_axis=0, tiled=True
    )
    key_full = keys_taken[:, :key_rows].reshape(key_count, head_width)
    value_full = keys_taken[:, key_rows:].reshape(key_count, head_width)
    ends = jnp.cumsum(lengths).astype(jnp.int32)
    dquery, terms = attend_kernel(
        query[0].reshape(tokens * head_count, head_width),
        out_grad[0].reshape(tokens * head_count, head_width),
        key_full,
        value_full,
        ends,
        own_index * tokens + iota * block_rows,
        head_count,
    )
    dquery = dquery.reshape(tokens, width)
    term_rows = tokens * 2 * head_width // width
    packed = jnp.concatenate(
        [reorder(dquery), terms.astype(jnp.bfloat16).reshape(shards, term_rows, width)], axis=1
    )
    received = lax.all_to_all(packed, "cp", split_axis=0, concat_axis=0, tiled=True)
    planned = received[:, :block_rows].reshape(tokens, width)
    handed = passed_along(planned, "pp", -1)
    partials = received[:, block_rows:].reshape(shards, tokens, 2 * head_width)
    summed = jnp.sum(partials.astype(jnp.float32), axis=0)
    key_grad = summed[:, :head_width].astype(jnp.bfloat16)
    value_grad = summed[:, head_width:].astype(jnp.bfloat16)
    return (handed[None], key_grad[None], value_grad[None])


def solution(mesh):
    return jax.shard_map(
        body,
        mesh=mesh,
        in_specs=(
            P("pp", "cp", "tp"),
            P("pp", "cp", "tp"),
            P("pp", "cp", "tp"),
            P("pp", "cp", "tp"),
            P(),
            P(),
        ),
        out_specs=(P("pp", "cp", "tp"), P("pp", "cp", "tp"), P("pp", "cp", "tp")),
        check_vma=False,
    )
```

```python
import functools

import jax
import jax.numpy as jnp
from jax import lax
from jax.sharding import PartitionSpec as P
from jax.experimental import pallas as pl
from jax.experimental.pallas import tpu as pltpu


def passed_along(array, axis, by):
    peers = lax.axis_size(axis)
    pairs = [(i, i + by) for i in range(peers) if 0 <= i + by < peers]
    return lax.ppermute(array, axis, pairs)


def _doc_of(ends_ref, position):
    doc = jnp.int32(0)
    for i in range(ends_ref.shape[0]):
        doc = doc + (position >= ends_ref[i]).astype(jnp.int32)
    return doc


def _attend_kernel(heads, kb_size, ends_ref, start_ref, kdoc_ref, q_ref, g_ref, k_ref, v_ref, dq_ref, dkv_ref, top_ref, total_ref, weighted_ref, dq_acc):
    rows, head_width = q_ref.shape
    keys = k_ref.shape[0]
    rb_size = rows // start_ref.shape[0]
    row_blocks = rows // rb_size
    key_blocks = keys // kb_size
    tokens_per_block = rb_size // heads
    scale = head_width ** (-0.5)
    dkv_ref[...] = jnp.zeros_like(dkv_ref)
    row_iota = lax.broadcasted_iota(jnp.int32, (rb_size, kb_size), 0) // heads
    col_iota = lax.broadcasted_iota(jnp.int32, (rb_size, kb_size), 1)
    row_iota1 = lax.broadcasted_iota(jnp.int32, (rb_size, 1), 0) // heads

    def vector_doc(position):
        doc = jnp.zeros(position.shape, jnp.int32)
        for i in range(ends_ref.shape[0]):
            doc = doc + (position >= ends_ref[i]).astype(jnp.int32)
        return doc

    def row_block(rb, carry):
        first = start_ref[rb]
        last = first + tokens_per_block - 1
        first_doc = _doc_of(ends_ref, first)
        last_doc = _doc_of(ends_ref, last)
        r0 = pl.multiple_of(rb * rb_size, rb_size)
        q = q_ref[pl.ds(r0, rb_size), :]
        g = g_ref[pl.ds(r0, rb_size), :]
        row_pos = first + row_iota
        row_doc = vector_doc(first + row_iota1)
        top_ref[...] = jnp.full(top_ref.shape, -1e30, jnp.float32)
        total_ref[...] = jnp.zeros(total_ref.shape, jnp.float32)
        weighted_ref[...] = jnp.zeros(weighted_ref.shape, jnp.float32)
        dq_acc[...] = jnp.zeros(dq_acc.shape, jnp.float32)

        def seen(kb):
            k0 = kb * kb_size
            return (k0 <= last) & (_doc_of(ends_ref, k0) <= last_doc) & (_doc_of(ends_ref, k0 + kb_size - 1) >= first_doc)

        def scores_of(kb):
            k0 = pl.multiple_of(kb * kb_size, kb_size)
            k = k_ref[pl.ds(k0, kb_size), :]
            v = v_ref[pl.ds(k0, kb_size), :]
            s = lax.dot_general(q, k, (((1,), (1,)), ((), ())), preferred_element_type=jnp.float32) * scale
            key_pos = k0 + col_iota
            key_doc = kdoc_ref[:, pl.ds(k0, kb_size)]
            visible = (key_doc == row_doc) & (key_pos <= row_pos)
            s = jnp.where(visible, s, -jnp.inf)
            dp = lax.dot_general(g, v, (((1,), (1,)), ((), ())), preferred_element_type=jnp.float32)
            return k0, k, s, dp

        def first_pass(kb, c):
            @pl.when(seen(kb))
            def _():
                _, _, s, dp = scores_of(kb)
                top = top_ref[...]
                new_top = jnp.maximum(top, jnp.max(s, axis=1, keepdims=True))
                expo = jnp.exp(s - new_top)
                shrink = jnp.exp(top - new_top)
                total_ref[...] = total_ref[...] * shrink + jnp.sum(expo, axis=1, keepdims=True)
                weighted_ref[...] = weighted_ref[...] * shrink + jnp.sum(expo * dp, axis=1, keepdims=True)
                top_ref[...] = new_top
            return c

        lax.fori_loop(0, key_blocks, first_pass, 0)
        top = top_ref[...]
        total = total_ref[...]
        delta = weighted_ref[...] / total
        inverse_total = 1.0 / total

        def second_pass(kb, c):
            @pl.when(seen(kb))
            def _():
                k0, k, s, dp = scores_of(kb)
                probs = jnp.exp(s - top) * inverse_total
                probs_low = probs.astype(jnp.bfloat16)
                dscore = (probs * (dp - delta) * scale).astype(jnp.bfloat16)
                dv = lax.dot_general(probs_low, g, (((0,), (0,)), ((), ())), preferred_element_type=jnp.float32)
                dk = lax.dot_general(dscore, q, (((0,), (0,)), ((), ())), preferred_element_type=jnp.float32)
                dkv_ref[pl.ds(k0, kb_size), pl.ds(0, head_width)] += dk
                dkv_ref[pl.ds(k0, kb_size), pl.ds(head_width, head_width)] += dv
                dq_acc[...] += jnp.dot(dscore, k, preferred_element_type=jnp.float32)
            return c

        lax.fori_loop(0, key_blocks, second_pass, 0)
        dq_ref[pl.ds(r0, rb_size), :] = dq_acc[...].astype(dq_ref.dtype)
        return carry

    lax.fori_loop(0, row_blocks, row_block, 0)


def attend_kernel(flat_query, flat_grad, key_full, value_full, ends, block_start, heads, kb_size=1024):
    rows, head_width = flat_query.shape
    keys = key_full.shape[0]
    rb_size = rows // block_start.shape[0]
    vmem = pltpu.VMEM
    smem = pl.BlockSpec(memory_space=pltpu.SMEM)
    whole = pl.BlockSpec(memory_space=pltpu.VMEM)
    flops = 2 * rows * keys * head_width * 7
    positions = jnp.arange(keys, dtype=jnp.int32)
    key_doc = jnp.sum((positions[:, None] >= ends[None, :]).astype(jnp.int32), axis=1)[None, :]
    return pl.pallas_call(
        functools.partial(_attend_kernel, heads, kb_size),
        out_shape=(
            jax.ShapeDtypeStruct((rows, head_width), jnp.bfloat16),
            jax.ShapeDtypeStruct((keys, 2 * head_width), jnp.float32),
        ),
        in_specs=[smem, smem, whole, whole, whole, whole, whole],
        out_specs=(whole, whole),
        scratch_shapes=[
            vmem((rb_size, 1), jnp.float32),
            vmem((rb_size, 1), jnp.float32),
            vmem((rb_size, 1), jnp.float32),
            vmem((rb_size, head_width), jnp.float32),
        ],
        compiler_params=pltpu.CompilerParams(vmem_limit_bytes=48 * 1024 * 1024),
        cost_estimate=pl.CostEstimate(flops=flops // 4, transcendentals=rows * keys // 2, bytes_accessed=rows * head_width * 6 + keys * head_width * 4 + keys * head_width * 8),
    )(ends, block_start, key_doc, flat_query, flat_grad, key_full, value_full)


def body(query, key, value, out_grad, lengths, plan):
    tokens = query.shape[1]
    width = query.shape[2]
    head_width = key.shape[2]
    head_count = width // head_width
    shards = lax.axis_size("cp")
    own_index = lax.axis_index("cp")
    block_rows = tokens // shards
    key_count = shards * tokens
    iota = jnp.arange(shards, dtype=jnp.int32)
    inverse = jnp.sum(
        (plan[:, None, :] == iota[None, :, None]).astype(jnp.int32) * iota[None, None, :], axis=2
    )
    send_order = lax.dynamic_index_in_dim(inverse, own_index, 0, keepdims=False)

    def reorder(rows):
        grouped = rows.reshape(shards, block_rows, rows.shape[1])
        return jnp.take(grouped, send_order, axis=0)

    key_rows = tokens * head_width // width
    own_keys = jnp.concatenate([key[0].reshape(key_rows, width), value[0].reshape(key_rows, width)], axis=0)
    keys_taken = lax.all_to_all(
        jnp.broadcast_to(own_keys[None], (shards,) + own_keys.shape), "cp", split_axis=0, concat_axis=0, tiled=True
    )
    key_full = keys_taken[:, :key_rows].reshape(key_count, head_width)
    value_full = keys_taken[:, key_rows:].reshape(key_count, head_width)
    ends = jnp.cumsum(lengths).astype(jnp.int32)
    dquery, terms = attend_kernel(
        query[0].reshape(tokens * head_count, head_width),
        out_grad[0].reshape(tokens * head_count, head_width),
        key_full,
        value_full,
        ends,
        own_index * tokens + iota * block_rows,
        head_count,
    )
    dquery = dquery.reshape(tokens, width)
    planned = lax.all_to_all(reorder(dquery), "cp", split_axis=0, concat_axis=0, tiled=True)
    handed = passed_along(planned.reshape(tokens, width), "pp", -1)
    partials = lax.all_to_all(
        terms.astype(jnp.bfloat16).reshape(shards, tokens, 2 * head_width), "cp", split_axis=0, concat_axis=0, tiled=True
    )
    summed = jnp.sum(partials.astype(jnp.float32), axis=0)
    key_grad = summed[:, :head_width].astype(jnp.bfloat16)
    value_grad = summed[:, head_width:].astype(jnp.bfloat16)
    return (handed[None], key_grad[None], value_grad[None])


def solution(mesh):
    return jax.shard_map(
        body,
        mesh=mesh,
        in_specs=(
            P("pp", "cp", "tp"),
            P("pp", "cp", "tp"),
            P("pp", "cp", "tp"),
            P("pp", "cp", "tp"),
            P(),
            P(),
        ),
        out_specs=(P("pp", "cp", "tp"), P("pp", "cp", "tp"), P("pp", "cp", "tp")),
        check_vma=False,
    )
```

```python
import functools

import jax
import jax.numpy as jnp
from jax import lax
from jax.sharding import PartitionSpec as P
from jax.experimental import pallas as pl
from jax.experimental.pallas import tpu as pltpu


def passed_along(array, axis, by):
    peers = lax.axis_size(axis)
    pairs = [(i, i + by) for i in range(peers) if 0 <= i + by < peers]
    return lax.ppermute(array, axis, pairs)


def _doc_of(ends_ref, position):
    doc = jnp.int32(0)
    for i in range(ends_ref.shape[0]):
        doc = doc + (position >= ends_ref[i]).astype(jnp.int32)
    return doc


def _attend_kernel(heads, kb_size, sub, ends_ref, start_ref, kdoc_ref, q_ref, g_ref, k_ref, v_ref, dq_ref, dkv_ref, top_ref, total_ref, weighted_ref, dq_acc):
    rows, head_width = q_ref.shape
    keys = k_ref.shape[0]
    piece = rows // start_ref.shape[0]
    rb_size = piece * sub
    row_blocks = rows // rb_size
    key_blocks = keys // kb_size
    tokens_per_block = piece // heads
    scale = head_width ** (-0.5)
    dkv_ref[...] = jnp.zeros_like(dkv_ref)
    row_raw = lax.broadcasted_iota(jnp.int32, (rb_size, kb_size), 0)
    row_iota = (row_raw % piece) // heads
    row_part = row_raw // piece
    col_iota = lax.broadcasted_iota(jnp.int32, (rb_size, kb_size), 1)

    def vector_doc(position):
        doc = jnp.zeros(position.shape, jnp.int32)
        for i in range(ends_ref.shape[0]):
            doc = doc + (position >= ends_ref[i]).astype(jnp.int32)
        return doc

    def row_block(rb, carry):
        firsts = [start_ref[rb * sub + i] for i in range(sub)]
        first_docs = [_doc_of(ends_ref, f) for f in firsts]
        last_docs = [_doc_of(ends_ref, f + tokens_per_block - 1) for f in firsts]
        r0 = pl.multiple_of(rb * rb_size, rb_size)
        q = q_ref[pl.ds(r0, rb_size), :]
        g = g_ref[pl.ds(r0, rb_size), :]
        row_first = firsts[0]
        for i in range(1, sub):
            row_first = jnp.where(row_part == i, firsts[i], row_first)
        row_pos = row_first + row_iota
        row_doc = vector_doc(row_pos)
        top_ref[...] = jnp.full(top_ref.shape, -1e30, jnp.float32)
        total_ref[...] = jnp.zeros(total_ref.shape, jnp.float32)
        weighted_ref[...] = jnp.zeros(weighted_ref.shape, jnp.float32)
        dq_acc[...] = jnp.zeros(dq_acc.shape, jnp.float32)

        def seen(kb):
            k0 = kb * kb_size
            k0_doc = _doc_of(ends_ref, k0)
            k1_doc = _doc_of(ends_ref, k0 + kb_size - 1)
            result = None
            for f, fd, ld in zip(firsts, first_docs, last_docs):
                one = (k0 <= f + tokens_per_block - 1) & (k0_doc <= ld) & (k1_doc >= fd)
                result = one if result is None else (result | one)
            return result

        def scores_of(kb):
            k0 = pl.multiple_of(kb * kb_size, kb_size)
            k = k_ref[pl.ds(k0, kb_size), :]
            v = v_ref[pl.ds(k0, kb_size), :]
            s = lax.dot_general(q, k, (((1,), (1,)), ((), ())), preferred_element_type=jnp.float32) * scale
            key_pos = k0 + col_iota
            key_doc = kdoc_ref[:, pl.ds(k0, kb_size)]
            visible = (key_doc == row_doc) & (key_pos <= row_pos)
            s = jnp.where(visible, s, -jnp.inf)
            dp = lax.dot_general(g, v, (((1,), (1,)), ((), ())), preferred_element_type=jnp.float32)
            return k0, k, s, dp

        def first_pass(kb, c):
            @pl.when(seen(kb))
            def _():
                _, _, s, dp = scores_of(kb)
                top = top_ref[...]
                new_top = jnp.maximum(top, jnp.max(s, axis=1, keepdims=True))
                expo = jnp.exp(s - new_top)
                shrink = jnp.exp(top - new_top)
                total_ref[...] = total_ref[...] * shrink + jnp.sum(expo, axis=1, keepdims=True)
                weighted_ref[...] = weighted_ref[...] * shrink + jnp.sum(expo * dp, axis=1, keepdims=True)
                top_ref[...] = new_top
            return c

        lax.fori_loop(0, key_blocks, first_pass, 0)
        top = top_ref[...]
        total = total_ref[...]
        delta = weighted_ref[...] / total
        inverse_total = 1.0 / total

        def second_pass(kb, c):
            @pl.when(seen(kb))
            def _():
                k0, k, s, dp = scores_of(kb)
                probs = jnp.exp(s - top) * inverse_total
                probs_low = probs.astype(jnp.bfloat16)
                dscore = (probs * (dp - delta) * scale).astype(jnp.bfloat16)
                dv = lax.dot_general(probs_low, g, (((0,), (0,)), ((), ())), preferred_element_type=jnp.float32)
                dk = lax.dot_general(dscore, q, (((0,), (0,)), ((), ())), preferred_element_type=jnp.float32)
                dkv_ref[pl.ds(k0, kb_size), pl.ds(0, head_width)] += dk
                dkv_ref[pl.ds(k0, kb_size), pl.ds(head_width, head_width)] += dv
                dq_acc[...] += jnp.dot(dscore, k, preferred_element_type=jnp.float32)
            return c

        lax.fori_loop(0, key_blocks, second_pass, 0)
        dq_ref[pl.ds(r0, rb_size), :] = dq_acc[...].astype(dq_ref.dtype)
        return carry

    lax.fori_loop(0, row_blocks, row_block, 0)


def attend_kernel(flat_query, flat_grad, key_full, value_full, ends, block_start, heads, kb_size=1024, sub=4):
    rows, head_width = flat_query.shape
    keys = key_full.shape[0]
    rb_size = rows // block_start.shape[0] * sub
    vmem = pltpu.VMEM
    smem = pl.BlockSpec(memory_space=pltpu.SMEM)
    whole = pl.BlockSpec(memory_space=pltpu.VMEM)
    flops = 2 * rows * keys * head_width * 7
    positions = jnp.arange(keys, dtype=jnp.int32)
    key_doc = jnp.sum((positions[:, None] >= ends[None, :]).astype(jnp.int32), axis=1)[None, :]
    return pl.pallas_call(
        functools.partial(_attend_kernel, heads, kb_size, sub),
        out_shape=(
            jax.ShapeDtypeStruct((rows, head_width), jnp.bfloat16),
            jax.ShapeDtypeStruct((keys, 2 * head_width), jnp.float32),
        ),
        in_specs=[smem, smem, whole, whole, whole, whole, whole],
        out_specs=(whole, whole),
        scratch_shapes=[
            vmem((rb_size, 1), jnp.float32),
            vmem((rb_size, 1), jnp.float32),
            vmem((rb_size, 1), jnp.float32),
            vmem((rb_size, head_width), jnp.float32),
        ],
        compiler_params=pltpu.CompilerParams(vmem_limit_bytes=48 * 1024 * 1024),
        cost_estimate=pl.CostEstimate(flops=flops // 4, transcendentals=rows * keys // 2, bytes_accessed=rows * head_width * 6 + keys * head_width * 4 + keys * head_width * 8),
    )(ends, block_start, key_doc, flat_query, flat_grad, key_full, value_full)


def body(query, key, value, out_grad, lengths, plan):
    tokens = query.shape[1]
    width = query.shape[2]
    head_width = key.shape[2]
    shards = lax.axis_size("cp")
    own_index = lax.axis_index("cp")
    block_rows = tokens // shards
    key_count = shards * tokens
    iota = jnp.arange(shards, dtype=jnp.int32)
    inverse = jnp.sum(
        (plan[:, None, :] == iota[None, :, None]).astype(jnp.int32) * iota[None, None, :], axis=2
    )
    send_order = lax.dynamic_index_in_dim(inverse, own_index, 0, keepdims=False)

    def reorder(rows):
        grouped = rows.reshape(shards, block_rows, rows.shape[1])
        return jnp.take(grouped, send_order, axis=0)

    key_rows = tokens * head_width // width
    own_keys = jnp.concatenate([key[0].reshape(key_rows, width), value[0].reshape(key_rows, width)], axis=0)
    packed = jnp.concatenate(
        [
            reorder(query[0]),
            reorder(out_grad[0]),
            jnp.broadcast_to(own_keys[None], (shards,) + own_keys.shape),
        ],
        axis=1,
    )
    received = lax.all_to_all(packed, "cp", split_axis=0, concat_axis=0, tiled=True)
    query_sent = received[:, :block_rows]
    grad_sent = received[:, block_rows : 2 * block_rows]
    key_at = 2 * block_rows
    key_full = received[:, key_at : key_at + key_rows].reshape(key_count, head_width)
    value_full = received[:, key_at + key_rows :].reshape(key_count, head_width)
    ends = jnp.cumsum(lengths).astype(jnp.int32)
    taken = lax.dynamic_index_in_dim(inverse, own_index, 1, keepdims=False)
    head_count = width // head_width
    dquery, terms = attend_kernel(
        query_sent.reshape(tokens * head_count, head_width),
        grad_sent.reshape(tokens * head_count, head_width),
        key_full,
        value_full,
        ends,
        iota * tokens + taken * block_rows,
        head_count,
    )
    dquery = dquery.reshape(tokens, width)
    handed = passed_along(dquery, "pp", -1)
    partials = lax.all_to_all(
        terms.astype(jnp.bfloat16).reshape(shards, tokens, 2 * head_width), "cp", split_axis=0, concat_axis=0, tiled=True
    )
    summed = jnp.sum(partials.astype(jnp.float32), axis=0)
    key_grad = summed[:, :head_width].astype(jnp.bfloat16)
    value_grad = summed[:, head_width:].astype(jnp.bfloat16)
    return (handed[None], key_grad[None], value_grad[None])


def solution(mesh):
    return jax.shard_map(
        body,
        mesh=mesh,
        in_specs=(
            P("pp", "cp", "tp"),
            P("pp", "cp", "tp"),
            P("pp", "cp", "tp"),
            P("pp", "cp", "tp"),
            P(),
            P(),
        ),
        out_specs=(P("pp", "cp", "tp"), P("pp", "cp", "tp"), P("pp", "cp", "tp")),
        check_vma=False,
    )
```

```python
import functools

import jax
import jax.numpy as jnp
from jax import lax
from jax.sharding import PartitionSpec as P
from jax.experimental import pallas as pl
from jax.experimental.pallas import tpu as pltpu


def passed_along(array, axis, by):
    peers = lax.axis_size(axis)
    pairs = [(i, i + by) for i in range(peers) if 0 <= i + by < peers]
    return lax.ppermute(array, axis, pairs)


def _doc_of(ends_ref, position):
    doc = jnp.int32(0)
    for i in range(ends_ref.shape[0]):
        doc = doc + (position >= ends_ref[i]).astype(jnp.int32)
    return doc


def _attend_kernel(heads, kb_size, sub, ends_ref, start_ref, kdoc_ref, q_ref, g_ref, k_ref, v_ref, dq_ref, dkv_ref, top_ref, total_ref, weighted_ref, dq_acc):
    rows, head_width = q_ref.shape
    keys = k_ref.shape[0]
    piece = rows // start_ref.shape[0]
    rb_size = piece * sub
    row_blocks = rows // rb_size
    key_blocks = keys // kb_size
    tokens_per_block = piece // heads
    scale = head_width ** (-0.5)
    dkv_ref[...] = jnp.zeros_like(dkv_ref)
    row_raw = lax.broadcasted_iota(jnp.int32, (rb_size, kb_size), 0)
    row_iota = (row_raw % piece) // heads
    row_part = row_raw // piece
    col_iota = lax.broadcasted_iota(jnp.int32, (rb_size, kb_size), 1)

    def vector_doc(position):
        doc = jnp.zeros(position.shape, jnp.int32)
        for i in range(ends_ref.shape[0]):
            doc = doc + (position >= ends_ref[i]).astype(jnp.int32)
        return doc

    def row_block(rb, carry):
        firsts = [start_ref[rb * sub + i] for i in range(sub)]
        first_docs = [_doc_of(ends_ref, f) for f in firsts]
        last_docs = [_doc_of(ends_ref, f + tokens_per_block - 1) for f in firsts]
        r0 = pl.multiple_of(rb * rb_size, rb_size)
        q = q_ref[pl.ds(r0, rb_size), :]
        g = g_ref[pl.ds(r0, rb_size), :]
        row_first = firsts[0]
        for i in range(1, sub):
            row_first = jnp.where(row_part == i, firsts[i], row_first)
        row_pos = row_first + row_iota
        row_doc = vector_doc(row_pos)
        top_ref[...] = jnp.full(top_ref.shape, -1e30, jnp.float32)
        total_ref[...] = jnp.zeros(total_ref.shape, jnp.float32)
        weighted_ref[...] = jnp.zeros(weighted_ref.shape, jnp.float32)
        dq_acc[...] = jnp.zeros(dq_acc.shape, jnp.float32)

        def seen(kb):
            k0 = kb * kb_size
            k0_doc = _doc_of(ends_ref, k0)
            k1_doc = _doc_of(ends_ref, k0 + kb_size - 1)
            result = None
            for f, fd, ld in zip(firsts, first_docs, last_docs):
                one = (k0 <= f + tokens_per_block - 1) & (k0_doc <= ld) & (k1_doc >= fd)
                result = one if result is None else (result | one)
            return result

        def scores_of(kb):
            k0 = pl.multiple_of(kb * kb_size, kb_size)
            k = k_ref[pl.ds(k0, kb_size), :]
            v = v_ref[pl.ds(k0, kb_size), :]
            s = lax.dot_general(q, k, (((1,), (1,)), ((), ())), preferred_element_type=jnp.float32) * scale
            key_pos = k0 + col_iota
            key_doc = kdoc_ref[:, pl.ds(k0, kb_size)]
            visible = (key_doc == row_doc) & (key_pos <= row_pos)
            s = jnp.where(visible, s, -jnp.inf)
            dp = lax.dot_general(g, v, (((1,), (1,)), ((), ())), preferred_element_type=jnp.float32)
            return k0, k, s, dp

        def first_pass(kb, c):
            @pl.when(seen(kb))
            def _():
                _, _, s, dp = scores_of(kb)
                top = top_ref[...]
                new_top = jnp.maximum(top, jnp.max(s, axis=1, keepdims=True))
                expo = jnp.exp(s - new_top)
                shrink = jnp.exp(top - new_top)
                total_ref[...] = total_ref[...] * shrink + jnp.sum(expo, axis=1, keepdims=True)
                weighted_ref[...] = weighted_ref[...] * shrink + jnp.sum(expo * dp, axis=1, keepdims=True)
                top_ref[...] = new_top
            return c

        lax.fori_loop(0, key_blocks, first_pass, 0)
        top = top_ref[...]
        total = total_ref[...]
        delta = weighted_ref[...] / total
        inverse_total = 1.0 / total

        def second_pass(kb, c):
            @pl.when(seen(kb))
            def _():
                k0, k, s, dp = scores_of(kb)
                probs = jnp.exp(s - top) * inverse_total
                probs_low = probs.astype(jnp.bfloat16)
                dscore = (probs * (dp - delta) * scale).astype(jnp.bfloat16)
                dv = lax.dot_general(probs_low, g, (((0,), (0,)), ((), ())), preferred_element_type=jnp.float32)
                dk = lax.dot_general(dscore, q, (((0,), (0,)), ((), ())), preferred_element_type=jnp.float32)
                dkv_ref[pl.ds(k0, kb_size), pl.ds(0, head_width)] += dk
                dkv_ref[pl.ds(k0, kb_size), pl.ds(head_width, head_width)] += dv
                dq_acc[...] += jnp.dot(dscore, k, preferred_element_type=jnp.float32)
            return c

        lax.fori_loop(0, key_blocks, second_pass, 0)
        dq_ref[pl.ds(r0, rb_size), :] = dq_acc[...].astype(dq_ref.dtype)
        return carry

    lax.fori_loop(0, row_blocks, row_block, 0)


def attend_kernel(flat_query, flat_grad, key_full, value_full, ends, block_start, heads, kb_size=1024, sub=4):
    rows, head_width = flat_query.shape
    keys = key_full.shape[0]
    rb_size = rows // block_start.shape[0] * sub
    vmem = pltpu.VMEM
    smem = pl.BlockSpec(memory_space=pltpu.SMEM)
    whole = pl.BlockSpec(memory_space=pltpu.VMEM)
    flops = 2 * rows * keys * head_width * 7
    positions = jnp.arange(keys, dtype=jnp.int32)
    key_doc = jnp.sum((positions[:, None] >= ends[None, :]).astype(jnp.int32), axis=1)[None, :]
    return pl.pallas_call(
        functools.partial(_attend_kernel, heads, kb_size, sub),
        out_shape=(
            jax.ShapeDtypeStruct((rows, head_width), jnp.bfloat16),
            jax.ShapeDtypeStruct((keys, 2 * head_width), jnp.float32),
        ),
        in_specs=[smem, smem, whole, whole, whole, whole, whole],
        out_specs=(whole, whole),
        scratch_shapes=[
            vmem((rb_size, 1), jnp.float32),
            vmem((rb_size, 1), jnp.float32),
            vmem((rb_size, 1), jnp.float32),
            vmem((rb_size, head_width), jnp.float32),
        ],
        compiler_params=pltpu.CompilerParams(vmem_limit_bytes=48 * 1024 * 1024),
        cost_estimate=pl.CostEstimate(flops=flops // 4, transcendentals=rows * keys // 2, bytes_accessed=rows * head_width * 6 + keys * head_width * 4 + keys * head_width * 8),
    )(ends, block_start, key_doc, flat_query, flat_grad, key_full, value_full)


def body(query, key, value, out_grad, lengths, plan):
    tokens = query.shape[1]
    width = query.shape[2]
    head_width = key.shape[2]
    shards = lax.axis_size("cp")
    own_index = lax.axis_index("cp")
    block_rows = tokens // shards
    key_count = shards * tokens
    iota = jnp.arange(shards, dtype=jnp.int32)
    inverse = jnp.sum(
        (plan[:, None, :] == iota[None, :, None]).astype(jnp.int32) * iota[None, None, :], axis=2
    )
    send_order = lax.dynamic_index_in_dim(inverse, own_index, 0, keepdims=False)

    def reorder(rows):
        grouped = rows.reshape(shards, block_rows, rows.shape[1])
        return jnp.take(grouped, send_order, axis=0)

    head_count = width // head_width
    piece = block_rows * head_count

    def as_heads(rows):
        return reorder(rows).reshape(shards, piece, head_width)

    own_keys = jnp.concatenate([key[0], value[0]], axis=0)
    packed = jnp.concatenate(
        [
            as_heads(query[0]),
            as_heads(out_grad[0]),
            jnp.broadcast_to(own_keys[None], (shards,) + own_keys.shape),
        ],
        axis=1,
    )
    received = lax.all_to_all(packed, "cp", split_axis=0, concat_axis=0, tiled=True)
    flat_query = received[:, :piece].reshape(shards * piece, head_width)
    flat_grad = received[:, piece : 2 * piece].reshape(shards * piece, head_width)
    key_at = 2 * piece
    key_full = received[:, key_at : key_at + tokens].reshape(key_count, head_width)
    value_full = received[:, key_at + tokens :].reshape(key_count, head_width)
    ends = jnp.cumsum(lengths).astype(jnp.int32)
    taken = lax.dynamic_index_in_dim(inverse, own_index, 1, keepdims=False)
    dquery, terms = attend_kernel(
        flat_query,
        flat_grad,
        key_full,
        value_full,
        ends,
        iota * tokens + taken * block_rows,
        head_count,
    )
    dquery = dquery.reshape(tokens, width)
    handed = passed_along(dquery, "pp", -1)
    partials = lax.all_to_all(
        terms.astype(jnp.bfloat16).reshape(shards, tokens, 2 * head_width), "cp", split_axis=0, concat_axis=0, tiled=True
    )
    summed = jnp.sum(partials.astype(jnp.float32), axis=0)
    key_grad = summed[:, :head_width].astype(jnp.bfloat16)
    value_grad = summed[:, head_width:].astype(jnp.bfloat16)
    return (handed[None], key_grad[None], value_grad[None])


def solution(mesh):
    return jax.shard_map(
        body,
        mesh=mesh,
        in_specs=(
            P("pp", "cp", "tp"),
            P("pp", "cp", "tp"),
            P("pp", "cp", "tp"),
            P("pp", "cp", "tp"),
            P(),
            P(),
        ),
        out_specs=(P("pp", "cp", "tp"), P("pp", "cp", "tp"), P("pp", "cp", "tp")),
        check_vma=False,
    )
```

```python
import functools

import jax
import jax.numpy as jnp
from jax import lax
from jax.sharding import PartitionSpec as P
from jax.experimental import pallas as pl
from jax.experimental.pallas import tpu as pltpu


def passed_along(array, axis, by):
    peers = lax.axis_size(axis)
    pairs = [(i, i + by) for i in range(peers) if 0 <= i + by < peers]
    return lax.ppermute(array, axis, pairs)


def _doc_of(ends_ref, position):
    doc = jnp.int32(0)
    for i in range(ends_ref.shape[0]):
        doc = doc + (position >= ends_ref[i]).astype(jnp.int32)
    return doc


def _attend_kernel(heads, kb_size, sub, ends_ref, start_ref, kdoc_ref, q_ref, g_ref, k_ref, v_ref, dq_ref, dkv_ref, top_ref, total_ref, weighted_ref, dq_acc, s_keep, dp_keep):
    rows, head_width = q_ref.shape
    keys = k_ref.shape[0]
    piece = rows // start_ref.shape[0]
    rb_size = piece * sub
    row_blocks = rows // rb_size
    key_blocks = keys // kb_size
    tokens_per_block = piece // heads
    scale = head_width ** (-0.5)
    dkv_ref[...] = jnp.zeros_like(dkv_ref)
    row_raw = lax.broadcasted_iota(jnp.int32, (rb_size, kb_size), 0)
    row_iota = (row_raw % piece) // heads
    row_part = row_raw // piece
    col_iota = lax.broadcasted_iota(jnp.int32, (rb_size, kb_size), 1)

    def vector_doc(position):
        doc = jnp.zeros(position.shape, jnp.int32)
        for i in range(ends_ref.shape[0]):
            doc = doc + (position >= ends_ref[i]).astype(jnp.int32)
        return doc

    def row_block(rb, carry):
        firsts = [start_ref[rb * sub + i] for i in range(sub)]
        first_docs = [_doc_of(ends_ref, f) for f in firsts]
        last_docs = [_doc_of(ends_ref, f + tokens_per_block - 1) for f in firsts]
        r0 = pl.multiple_of(rb * rb_size, rb_size)
        q = q_ref[pl.ds(r0, rb_size), :]
        g = g_ref[pl.ds(r0, rb_size), :]
        row_first = firsts[0]
        for i in range(1, sub):
            row_first = jnp.where(row_part == i, firsts[i], row_first)
        row_pos = row_first + row_iota
        row_doc = vector_doc(row_pos)
        top_ref[...] = jnp.full(top_ref.shape, -1e30, jnp.float32)
        total_ref[...] = jnp.zeros(total_ref.shape, jnp.float32)
        weighted_ref[...] = jnp.zeros(weighted_ref.shape, jnp.float32)
        dq_acc[...] = jnp.zeros(dq_acc.shape, jnp.float32)

        def seen(kb):
            k0 = kb * kb_size
            k0_doc = _doc_of(ends_ref, k0)
            k1_doc = _doc_of(ends_ref, k0 + kb_size - 1)
            result = None
            for f, fd, ld in zip(firsts, first_docs, last_docs):
                one = (k0 <= f + tokens_per_block - 1) & (k0_doc <= ld) & (k1_doc >= fd)
                result = one if result is None else (result | one)
            return result

        def scores_of(kb):
            k0 = pl.multiple_of(kb * kb_size, kb_size)
            k = k_ref[pl.ds(k0, kb_size), :]
            v = v_ref[pl.ds(k0, kb_size), :]
            s = lax.dot_general(q, k, (((1,), (1,)), ((), ())), preferred_element_type=jnp.float32) * scale
            key_pos = k0 + col_iota
            key_doc = kdoc_ref[:, pl.ds(k0, kb_size)]
            visible = (key_doc == row_doc) & (key_pos <= row_pos)
            s = jnp.where(visible, s, -jnp.inf)
            dp = lax.dot_general(g, v, (((1,), (1,)), ((), ())), preferred_element_type=jnp.float32)
            return k0, k, s, dp

        def first_pass(kb, c):
            @pl.when(seen(kb))
            def _():
                _, _, s, dp = scores_of(kb)
                s_keep[kb] = s
                dp_keep[kb] = dp
                top = top_ref[...]
                new_top = jnp.maximum(top, jnp.max(s, axis=1, keepdims=True))
                expo = jnp.exp(s - new_top)
                shrink = jnp.exp(top - new_top)
                total_ref[...] = total_ref[...] * shrink + jnp.sum(expo, axis=1, keepdims=True)
                weighted_ref[...] = weighted_ref[...] * shrink + jnp.sum(expo * dp, axis=1, keepdims=True)
                top_ref[...] = new_top
            return c

        lax.fori_loop(0, key_blocks, first_pass, 0)
        top = top_ref[...]
        total = total_ref[...]
        delta = weighted_ref[...] / total
        inverse_total = 1.0 / total

        def second_pass(kb, c):
            @pl.when(seen(kb))
            def _():
                k0 = pl.multiple_of(kb * kb_size, kb_size)
                k = k_ref[pl.ds(k0, kb_size), :]
                s = s_keep[kb]
                dp = dp_keep[kb]
                probs = jnp.exp(s - top) * inverse_total
                probs_low = probs.astype(jnp.bfloat16)
                dscore = (probs * (dp - delta) * scale).astype(jnp.bfloat16)
                dv = lax.dot_general(probs_low, g, (((0,), (0,)), ((), ())), preferred_element_type=jnp.float32)
                dk = lax.dot_general(dscore, q, (((0,), (0,)), ((), ())), preferred_element_type=jnp.float32)
                dkv_ref[pl.ds(k0, kb_size), pl.ds(0, head_width)] += dk
                dkv_ref[pl.ds(k0, kb_size), pl.ds(head_width, head_width)] += dv
                dq_acc[...] += jnp.dot(dscore, k, preferred_element_type=jnp.float32)
            return c

        lax.fori_loop(0, key_blocks, second_pass, 0)
        dq_ref[pl.ds(r0, rb_size), :] = dq_acc[...].astype(dq_ref.dtype)
        return carry

    lax.fori_loop(0, row_blocks, row_block, 0)


def attend_kernel(flat_query, flat_grad, key_full, value_full, ends, block_start, heads, kb_size=1024, sub=4):
    rows, head_width = flat_query.shape
    keys = key_full.shape[0]
    rb_size = rows // block_start.shape[0] * sub
    vmem = pltpu.VMEM
    smem = pl.BlockSpec(memory_space=pltpu.SMEM)
    whole = pl.BlockSpec(memory_space=pltpu.VMEM)
    flops = 2 * rows * keys * head_width * 7
    positions = jnp.arange(keys, dtype=jnp.int32)
    key_doc = jnp.sum((positions[:, None] >= ends[None, :]).astype(jnp.int32), axis=1)[None, :]
    return pl.pallas_call(
        functools.partial(_attend_kernel, heads, kb_size, sub),
        out_shape=(
            jax.ShapeDtypeStruct((rows, head_width), jnp.bfloat16),
            jax.ShapeDtypeStruct((keys, 2 * head_width), jnp.float32),
        ),
        in_specs=[smem, smem, whole, whole, whole, whole, whole],
        out_specs=(whole, whole),
        scratch_shapes=[
            vmem((rb_size, 1), jnp.float32),
            vmem((rb_size, 1), jnp.float32),
            vmem((rb_size, 1), jnp.float32),
            vmem((rb_size, head_width), jnp.float32),
            vmem((keys // kb_size, rb_size, kb_size), jnp.float32),
            vmem((keys // kb_size, rb_size, kb_size), jnp.float32),
        ],
        compiler_params=pltpu.CompilerParams(vmem_limit_bytes=48 * 1024 * 1024),
        cost_estimate=pl.CostEstimate(flops=flops // 4, transcendentals=rows * keys // 2, bytes_accessed=rows * head_width * 6 + keys * head_width * 4 + keys * head_width * 8),
    )(ends, block_start, key_doc, flat_query, flat_grad, key_full, value_full)


def body(query, key, value, out_grad, lengths, plan):
    tokens = query.shape[1]
    width = query.shape[2]
    head_width = key.shape[2]
    shards = lax.axis_size("cp")
    own_index = lax.axis_index("cp")
    block_rows = tokens // shards
    key_count = shards * tokens
    iota = jnp.arange(shards, dtype=jnp.int32)
    inverse = jnp.sum(
        (plan[:, None, :] == iota[None, :, None]).astype(jnp.int32) * iota[None, None, :], axis=2
    )
    send_order = lax.dynamic_index_in_dim(inverse, own_index, 0, keepdims=False)

    def reorder(rows):
        grouped = rows.reshape(shards, block_rows, rows.shape[1])
        return jnp.take(grouped, send_order, axis=0)

    head_count = width // head_width
    piece = block_rows * head_count

    def as_heads(rows):
        return reorder(rows).reshape(shards, piece, head_width)

    own_keys = jnp.concatenate([key[0], value[0]], axis=0)
    packed = jnp.concatenate(
        [
            as_heads(query[0]),
            as_heads(out_grad[0]),
            jnp.broadcast_to(own_keys[None], (shards,) + own_keys.shape),
        ],
        axis=1,
    )
    received = lax.all_to_all(packed, "cp", split_axis=0, concat_axis=0, tiled=True)
    flat_query = received[:, :piece].reshape(shards * piece, head_width)
    flat_grad = received[:, piece : 2 * piece].reshape(shards * piece, head_width)
    key_at = 2 * piece
    key_full = received[:, key_at : key_at + tokens].reshape(key_count, head_width)
    value_full = received[:, key_at + tokens :].reshape(key_count, head_width)
    ends = jnp.cumsum(lengths).astype(jnp.int32)
    taken = lax.dynamic_index_in_dim(inverse, own_index, 1, keepdims=False)
    dquery, terms = attend_kernel(
        flat_query,
        flat_grad,
        key_full,
        value_full,
        ends,
        iota * tokens + taken * block_rows,
        head_count,
    )
    dquery = dquery.reshape(tokens, width)
    handed = passed_along(dquery, "pp", -1)
    partials = lax.all_to_all(
        terms.astype(jnp.bfloat16).reshape(shards, tokens, 2 * head_width), "cp", split_axis=0, concat_axis=0, tiled=True
    )
    summed = jnp.sum(partials.astype(jnp.float32), axis=0)
    key_grad = summed[:, :head_width].astype(jnp.bfloat16)
    value_grad = summed[:, head_width:].astype(jnp.bfloat16)
    return (handed[None], key_grad[None], value_grad[None])


def solution(mesh):
    return jax.shard_map(
        body,
        mesh=mesh,
        in_specs=(
            P("pp", "cp", "tp"),
            P("pp", "cp", "tp"),
            P("pp", "cp", "tp"),
            P("pp", "cp", "tp"),
            P(),
            P(),
        ),
        out_specs=(P("pp", "cp", "tp"), P("pp", "cp", "tp"), P("pp", "cp", "tp")),
        check_vma=False,
    )
```

```python
import functools

import jax
import jax.numpy as jnp
from jax import lax
from jax.sharding import PartitionSpec as P
from jax.experimental import pallas as pl
from jax.experimental.pallas import tpu as pltpu


def passed_along(array, axis, by):
    peers = lax.axis_size(axis)
    pairs = [(i, i + by) for i in range(peers) if 0 <= i + by < peers]
    return lax.ppermute(array, axis, pairs)


def _doc_of(ends_ref, position):
    doc = jnp.int32(0)
    for i in range(ends_ref.shape[0]):
        doc = doc + (position >= ends_ref[i]).astype(jnp.int32)
    return doc


def _attend_kernel(heads, kb_size, sub, ends_ref, start_ref, kdoc_ref, q_ref, g_ref, k_ref, v_ref, dq_ref, dkv_ref, top_ref, total_ref, weighted_ref, dq_acc, s_keep, dp_keep, m_keep, dkv_acc):
    rows, head_width = q_ref.shape
    keys = k_ref.shape[0]
    piece = rows // start_ref.shape[0]
    rb_size = piece * sub
    row_blocks = rows // rb_size
    key_blocks = keys // kb_size
    tokens_per_block = piece // heads
    scale = head_width ** (-0.5)
    dkv_acc[...] = jnp.zeros_like(dkv_acc)
    row_raw = lax.broadcasted_iota(jnp.int32, (rb_size, kb_size), 0)
    row_iota = (row_raw % piece) // heads
    row_part = row_raw // piece
    col_iota = lax.broadcasted_iota(jnp.int32, (rb_size, kb_size), 1)

    def vector_doc(position):
        doc = jnp.zeros(position.shape, jnp.int32)
        for i in range(ends_ref.shape[0]):
            doc = doc + (position >= ends_ref[i]).astype(jnp.int32)
        return doc

    def row_block(rb, carry):
        firsts = [start_ref[rb * sub + i] for i in range(sub)]
        first_docs = [_doc_of(ends_ref, f) for f in firsts]
        last_docs = [_doc_of(ends_ref, f + tokens_per_block - 1) for f in firsts]
        r0 = pl.multiple_of(rb * rb_size, rb_size)
        q = q_ref[pl.ds(r0, rb_size), :]
        g = g_ref[pl.ds(r0, rb_size), :]
        row_first = firsts[0]
        for i in range(1, sub):
            row_first = jnp.where(row_part == i, firsts[i], row_first)
        row_pos = row_first + row_iota
        row_doc = vector_doc(row_pos)
        top_ref[...] = jnp.full(top_ref.shape, -1e30, jnp.float32)
        total_ref[...] = jnp.zeros(total_ref.shape, jnp.float32)
        weighted_ref[...] = jnp.zeros(weighted_ref.shape, jnp.float32)
        dq_acc[...] = jnp.zeros(dq_acc.shape, jnp.float32)

        def seen(kb):
            k0 = kb * kb_size
            k0_doc = _doc_of(ends_ref, k0)
            k1_doc = _doc_of(ends_ref, k0 + kb_size - 1)
            result = None
            for f, fd, ld in zip(firsts, first_docs, last_docs):
                one = (k0 <= f + tokens_per_block - 1) & (k0_doc <= ld) & (k1_doc >= fd)
                result = one if result is None else (result | one)
            return result

        def scores_of(kb):
            k0 = pl.multiple_of(kb * kb_size, kb_size)
            k = k_ref[pl.ds(k0, kb_size), :]
            v = v_ref[pl.ds(k0, kb_size), :]
            s = lax.dot_general(q, k, (((1,), (1,)), ((), ())), preferred_element_type=jnp.float32) * scale
            key_pos = k0 + col_iota
            key_doc = kdoc_ref[:, pl.ds(k0, kb_size)]
            visible = (key_doc == row_doc) & (key_pos <= row_pos)
            s = jnp.where(visible, s, -jnp.inf)
            dp = lax.dot_general(g, v, (((1,), (1,)), ((), ())), preferred_element_type=jnp.float32)
            return k0, k, s, dp

        def first_pass(kb, c):
            @pl.when(seen(kb))
            def _():
                _, _, s, dp = scores_of(kb)
                dp_keep[kb] = dp
                top = top_ref[...]
                new_top = jnp.maximum(top, jnp.max(s, axis=1, keepdims=True))
                expo = jnp.exp(s - new_top)
                s_keep[kb] = expo
                m_keep[kb] = new_top
                shrink = jnp.exp(top - new_top)
                total_ref[...] = total_ref[...] * shrink + jnp.sum(expo, axis=1, keepdims=True)
                weighted_ref[...] = weighted_ref[...] * shrink + jnp.sum(expo * dp, axis=1, keepdims=True)
                top_ref[...] = new_top
            return c

        lax.fori_loop(0, key_blocks, first_pass, 0)
        top = top_ref[...]
        total = total_ref[...]
        delta = weighted_ref[...] / total
        inverse_total = 1.0 / total

        def second_pass(kb, c):
            @pl.when(seen(kb))
            def _():
                k0 = pl.multiple_of(kb * kb_size, kb_size)
                k = k_ref[pl.ds(k0, kb_size), :]
                dp = dp_keep[kb]
                probs = s_keep[kb] * (jnp.exp(m_keep[kb] - top) * inverse_total)
                probs_low = probs.astype(jnp.bfloat16)
                dscore = (probs * (dp - delta) * scale).astype(jnp.bfloat16)
                dv = lax.dot_general(probs_low, g, (((0,), (0,)), ((), ())), preferred_element_type=jnp.float32)
                dk = lax.dot_general(dscore, q, (((0,), (0,)), ((), ())), preferred_element_type=jnp.float32)
                dkv_acc[pl.ds(k0, kb_size), pl.ds(0, head_width)] += dk
                dkv_acc[pl.ds(k0, kb_size), pl.ds(head_width, head_width)] += dv
                dq_acc[...] += jnp.dot(dscore, k, preferred_element_type=jnp.float32)
            return c

        lax.fori_loop(0, key_blocks, second_pass, 0)
        dq_ref[pl.ds(r0, rb_size), :] = dq_acc[...].astype(dq_ref.dtype)
        return carry

    lax.fori_loop(0, row_blocks, row_block, 0)
    dkv_ref[...] = dkv_acc[...].astype(dkv_ref.dtype)


def attend_kernel(flat_query, flat_grad, key_full, value_full, ends, block_start, heads, kb_size=1024, sub=4):
    rows, head_width = flat_query.shape
    keys = key_full.shape[0]
    rb_size = rows // block_start.shape[0] * sub
    vmem = pltpu.VMEM
    smem = pl.BlockSpec(memory_space=pltpu.SMEM)
    whole = pl.BlockSpec(memory_space=pltpu.VMEM)
    flops = 2 * rows * keys * head_width * 7
    positions = jnp.arange(keys, dtype=jnp.int32)
    key_doc = jnp.sum((positions[:, None] >= ends[None, :]).astype(jnp.int32), axis=1)[None, :]
    return pl.pallas_call(
        functools.partial(_attend_kernel, heads, kb_size, sub),
        out_shape=(
            jax.ShapeDtypeStruct((rows, head_width), jnp.bfloat16),
            jax.ShapeDtypeStruct((keys, 2 * head_width), jnp.bfloat16),
        ),
        in_specs=[smem, smem, whole, whole, whole, whole, whole],
        out_specs=(whole, whole),
        scratch_shapes=[
            vmem((rb_size, 1), jnp.float32),
            vmem((rb_size, 1), jnp.float32),
            vmem((rb_size, 1), jnp.float32),
            vmem((rb_size, head_width), jnp.float32),
            vmem((keys // kb_size, rb_size, kb_size), jnp.float32),
            vmem((keys // kb_size, rb_size, kb_size), jnp.float32),
            vmem((keys // kb_size, rb_size, 1), jnp.float32),
            vmem((keys, 2 * head_width), jnp.float32),
        ],
        compiler_params=pltpu.CompilerParams(vmem_limit_bytes=48 * 1024 * 1024),
        cost_estimate=pl.CostEstimate(flops=flops // 4, transcendentals=rows * keys // 2, bytes_accessed=rows * head_width * 6 + keys * head_width * 4 + keys * head_width * 8),
    )(ends, block_start, key_doc, flat_query, flat_grad, key_full, value_full)


def body(query, key, value, out_grad, lengths, plan):
    tokens = query.shape[1]
    width = query.shape[2]
    head_width = key.shape[2]
    shards = lax.axis_size("cp")
    own_index = lax.axis_index("cp")
    block_rows = tokens // shards
    key_count = shards * tokens
    iota = jnp.arange(shards, dtype=jnp.int32)
    own_plan = lax.dynamic_index_in_dim(plan, own_index, 0, keepdims=False)
    send_order = jnp.sum((own_plan[None, :] == iota[:, None]).astype(jnp.int32) * iota[None, :], axis=1)
    taken = jnp.sum((plan == own_index).astype(jnp.int32) * iota[None, :], axis=1)

    def reorder(rows):
        grouped = rows.reshape(shards, block_rows, rows.shape[1])
        return jnp.take(grouped, send_order, axis=0)

    head_count = width // head_width
    piece = block_rows * head_count

    def as_heads(rows):
        return reorder(rows).reshape(shards, piece, head_width)

    own_keys = jnp.concatenate([key[0], value[0]], axis=0)
    packed = jnp.concatenate(
        [
            as_heads(query[0]),
            as_heads(out_grad[0]),
            jnp.broadcast_to(own_keys[None], (shards,) + own_keys.shape),
        ],
        axis=1,
    )
    received = lax.all_to_all(packed, "cp", split_axis=0, concat_axis=0, tiled=True)
    flat_query = received[:, :piece].reshape(shards * piece, head_width)
    flat_grad = received[:, piece : 2 * piece].reshape(shards * piece, head_width)
    key_at = 2 * piece
    key_full = received[:, key_at : key_at + tokens].reshape(key_count, head_width)
    value_full = received[:, key_at + tokens :].reshape(key_count, head_width)
    ends = jnp.cumsum(lengths).astype(jnp.int32)
    dquery, terms = attend_kernel(
        flat_query,
        flat_grad,
        key_full,
        value_full,
        ends,
        iota * tokens + taken * block_rows,
        head_count,
    )
    dquery = dquery.reshape(tokens, width)
    handed = passed_along(dquery, "pp", -1)
    partials = lax.all_to_all(
        terms.reshape(shards, tokens, 2 * head_width), "cp", split_axis=0, concat_axis=0, tiled=True
    )
    summed = jnp.sum(partials.astype(jnp.float32), axis=0)
    key_grad = summed[:, :head_width].astype(jnp.bfloat16)
    value_grad = summed[:, head_width:].astype(jnp.bfloat16)
    return (handed[None], key_grad[None], value_grad[None])


def solution(mesh):
    return jax.shard_map(
        body,
        mesh=mesh,
        in_specs=(
            P("pp", "cp", "tp"),
            P("pp", "cp", "tp"),
            P("pp", "cp", "tp"),
            P("pp", "cp", "tp"),
            P(),
            P(),
        ),
        out_specs=(P("pp", "cp", "tp"), P("pp", "cp", "tp"), P("pp", "cp", "tp")),
        check_vma=False,
    )
```

```python
import functools

import jax
import jax.numpy as jnp
from jax import lax
from jax.sharding import PartitionSpec as P
from jax.experimental import pallas as pl
from jax.experimental.pallas import tpu as pltpu


def passed_along(array, axis, by):
    peers = lax.axis_size(axis)
    pairs = [(i, i + by) for i in range(peers) if 0 <= i + by < peers]
    return lax.ppermute(array, axis, pairs)


def _doc_of(ends_ref, position):
    doc = jnp.int32(0)
    for i in range(ends_ref.shape[0]):
        doc = doc + (position >= ends_ref[i]).astype(jnp.int32)
    return doc


def _attend_kernel(heads, kb_size, sub, ends_ref, start_ref, kdoc_ref, q_ref, g_ref, k_ref, v_ref, dq_ref, dkv_ref, top_ref, total_ref, weighted_ref, dq_acc, s_keep, dp_keep, dkv_acc):
    rows, head_width = q_ref.shape
    keys = k_ref.shape[0]
    piece = rows // start_ref.shape[0]
    rb_size = piece * sub
    row_blocks = rows // rb_size
    key_blocks = keys // kb_size
    tokens_per_block = piece // heads
    scale = head_width ** (-0.5)
    dkv_acc[...] = jnp.zeros_like(dkv_acc)
    row_raw = lax.broadcasted_iota(jnp.int32, (rb_size, kb_size), 0)
    row_iota = (row_raw % piece) // heads
    row_part = row_raw // piece
    col_iota = lax.broadcasted_iota(jnp.int32, (rb_size, kb_size), 1)

    def vector_doc(position):
        doc = jnp.zeros(position.shape, jnp.int32)
        for i in range(ends_ref.shape[0]):
            doc = doc + (position >= ends_ref[i]).astype(jnp.int32)
        return doc

    def row_block(rb, carry):
        firsts = [start_ref[rb * sub + i] for i in range(sub)]
        first_docs = [_doc_of(ends_ref, f) for f in firsts]
        last_docs = [_doc_of(ends_ref, f + tokens_per_block - 1) for f in firsts]
        r0 = pl.multiple_of(rb * rb_size, rb_size)
        q = q_ref[pl.ds(r0, rb_size), :]
        g = g_ref[pl.ds(r0, rb_size), :]
        row_first = firsts[0]
        for i in range(1, sub):
            row_first = jnp.where(row_part == i, firsts[i], row_first)
        row_pos = row_first + row_iota
        row_doc = vector_doc(row_pos)
        top_ref[...] = jnp.full(top_ref.shape, -1e30, jnp.float32)
        total_ref[...] = jnp.zeros(total_ref.shape, jnp.float32)
        weighted_ref[...] = jnp.zeros(weighted_ref.shape, jnp.float32)
        dq_acc[...] = jnp.zeros(dq_acc.shape, jnp.float32)

        def seen(kb):
            k0 = kb * kb_size
            k0_doc = _doc_of(ends_ref, k0)
            k1_doc = _doc_of(ends_ref, k0 + kb_size - 1)
            result = None
            for f, fd, ld in zip(firsts, first_docs, last_docs):
                one = (k0 <= f + tokens_per_block - 1) & (k0_doc <= ld) & (k1_doc >= fd)
                result = one if result is None else (result | one)
            return result

        def scores_of(kb):
            k0 = pl.multiple_of(kb * kb_size, kb_size)
            k = k_ref[pl.ds(k0, kb_size), :]
            v = v_ref[pl.ds(k0, kb_size), :]
            s = lax.dot_general(q, k, (((1,), (1,)), ((), ())), preferred_element_type=jnp.float32) * scale
            key_pos = k0 + col_iota
            key_doc = kdoc_ref[:, pl.ds(k0, kb_size)]
            visible = (key_doc == row_doc) & (key_pos <= row_pos)
            s = jnp.where(visible, s, -jnp.inf)
            dp = lax.dot_general(g, v, (((1,), (1,)), ((), ())), preferred_element_type=jnp.float32)
            return k0, k, s, dp

        def first_pass(kb, c):
            @pl.when(seen(kb))
            def _():
                _, _, s, dp = scores_of(kb)
                s_keep[kb] = s
                dp_keep[kb] = dp
                top = top_ref[...]
                new_top = jnp.maximum(top, jnp.max(s, axis=1, keepdims=True))
                expo = jnp.exp(s - new_top)
                shrink = jnp.exp(top - new_top)
                total_ref[...] = total_ref[...] * shrink + jnp.sum(expo, axis=1, keepdims=True)
                weighted_ref[...] = weighted_ref[...] * shrink + jnp.sum(expo * dp, axis=1, keepdims=True)
                top_ref[...] = new_top
            return c

        lax.fori_loop(0, key_blocks, first_pass, 0)
        top = top_ref[...]
        total = total_ref[...]
        delta = weighted_ref[...] / total
        inverse_total = 1.0 / total

        def second_pass(kb, c):
            @pl.when(seen(kb))
            def _():
                k0 = pl.multiple_of(kb * kb_size, kb_size)
                k = k_ref[pl.ds(k0, kb_size), :]
                s = s_keep[kb]
                dp = dp_keep[kb]
                probs = jnp.exp(s - top) * inverse_total
                probs_low = probs.astype(jnp.bfloat16)
                dscore = (probs * (dp - delta) * scale).astype(jnp.bfloat16)
                dv = lax.dot_general(probs_low, g, (((0,), (0,)), ((), ())), preferred_element_type=jnp.float32)
                dk = lax.dot_general(dscore, q, (((0,), (0,)), ((), ())), preferred_element_type=jnp.float32)
                dkv_acc[pl.ds(k0, kb_size), pl.ds(0, head_width)] += dk
                dkv_acc[pl.ds(k0, kb_size), pl.ds(head_width, head_width)] += dv
                dq_acc[...] += jnp.dot(dscore, k, preferred_element_type=jnp.float32)
            return c

        lax.fori_loop(0, key_blocks, second_pass, 0)
        dq_ref[pl.ds(r0, rb_size), :] = dq_acc[...].astype(dq_ref.dtype)
        return carry

    lax.fori_loop(0, row_blocks, row_block, 0)
    dkv_ref[...] = dkv_acc[...].astype(dkv_ref.dtype)


def attend_kernel(flat_query, flat_grad, key_full, value_full, ends, block_start, heads, kb_size=1024, sub=4):
    rows, head_width = flat_query.shape
    keys = key_full.shape[0]
    rb_size = rows // block_start.shape[0] * sub
    vmem = pltpu.VMEM
    smem = pl.BlockSpec(memory_space=pltpu.SMEM)
    whole = pl.BlockSpec(memory_space=pltpu.VMEM)
    flops = 2 * rows * keys * head_width * 7
    positions = jnp.arange(keys, dtype=jnp.int32)
    key_doc = jnp.sum((positions[:, None] >= ends[None, :]).astype(jnp.int32), axis=1)[None, :]
    return pl.pallas_call(
        functools.partial(_attend_kernel, heads, kb_size, sub),
        out_shape=(
            jax.ShapeDtypeStruct((rows, head_width), jnp.bfloat16),
            jax.ShapeDtypeStruct((keys, 2 * head_width), jnp.bfloat16),
        ),
        in_specs=[smem, smem, whole, whole, whole, whole, whole],
        out_specs=(whole, whole),
        scratch_shapes=[
            vmem((rb_size, 1), jnp.float32),
            vmem((rb_size, 1), jnp.float32),
            vmem((rb_size, 1), jnp.float32),
            vmem((rb_size, head_width), jnp.float32),
            vmem((keys // kb_size, rb_size, kb_size), jnp.float32),
            vmem((keys // kb_size, rb_size, kb_size), jnp.float32),
            vmem((keys, 2 * head_width), jnp.float32),
        ],
        compiler_params=pltpu.CompilerParams(vmem_limit_bytes=48 * 1024 * 1024),
        cost_estimate=pl.CostEstimate(flops=flops // 4, transcendentals=rows * keys // 2, bytes_accessed=rows * head_width * 6 + keys * head_width * 4 + keys * head_width * 8),
    )(ends, block_start, key_doc, flat_query, flat_grad, key_full, value_full)


def body(query, key, value, out_grad, lengths, plan):
    tokens = query.shape[1]
    width = query.shape[2]
    head_width = key.shape[2]
    shards = lax.axis_size("cp")
    own_index = lax.axis_index("cp")
    block_rows = tokens // shards
    key_count = shards * tokens
    iota = jnp.arange(shards, dtype=jnp.int32)
    inverse = jnp.sum(
        (plan[:, None, :] == iota[None, :, None]).astype(jnp.int32) * iota[None, None, :], axis=2
    )
    send_order = lax.dynamic_index_in_dim(inverse, own_index, 0, keepdims=False)

    def reorder(rows):
        grouped = rows.reshape(shards, block_rows, rows.shape[1])
        return jnp.take(grouped, send_order, axis=0)

    head_count = width // head_width
    piece = block_rows * head_count

    def as_heads(rows):
        return reorder(rows).reshape(shards, piece, head_width)

    own_keys = jnp.concatenate([key[0], value[0]], axis=0)
    packed = jnp.concatenate(
        [
            as_heads(query[0]),
            as_heads(out_grad[0]),
            jnp.broadcast_to(own_keys[None], (shards,) + own_keys.shape),
        ],
        axis=1,
    )
    received = lax.all_to_all(packed, "cp", split_axis=0, concat_axis=0, tiled=True)
    flat_query = received[:, :piece].reshape(shards * piece, head_width)
    flat_grad = received[:, piece : 2 * piece].reshape(shards * piece, head_width)
    key_at = 2 * piece
    key_full = received[:, key_at : key_at + tokens].reshape(key_count, head_width)
    value_full = received[:, key_at + tokens :].reshape(key_count, head_width)
    ends = jnp.cumsum(lengths).astype(jnp.int32)
    taken = lax.dynamic_index_in_dim(inverse, own_index, 1, keepdims=False)
    dquery, terms = attend_kernel(
        flat_query,
        flat_grad,
        key_full,
        value_full,
        ends,
        iota * tokens + taken * block_rows,
        head_count,
    )
    handed = passed_along(dquery.reshape(1, tokens, width), "pp", -1)
    partials = lax.all_to_all(
        terms.reshape(shards, tokens, 2 * head_width), "cp", split_axis=0, concat_axis=0, tiled=True
    )
    key_grad = jnp.sum(partials[:, :, :head_width].astype(jnp.float32), axis=0).astype(jnp.bfloat16)
    value_grad = jnp.sum(partials[:, :, head_width:].astype(jnp.float32), axis=0).astype(jnp.bfloat16)
    return (handed, key_grad[None], value_grad[None])


def solution(mesh):
    return jax.shard_map(
        body,
        mesh=mesh,
        in_specs=(
            P("pp", "cp", "tp"),
            P("pp", "cp", "tp"),
            P("pp", "cp", "tp"),
            P("pp", "cp", "tp"),
            P(),
            P(),
        ),
        out_specs=(P("pp", "cp", "tp"), P("pp", "cp", "tp"), P("pp", "cp", "tp")),
        check_vma=False,
    )
```
